128 devices in a mesh: section: 8 (over x, core), expert: 16 (over z, y).
Axes of the slice: x: 4, y: 4, z: 4, core: 2. Of those that a mesh axis runs over, the one named last changes fastest.
Arguments:
- inputs: bfloat16 [4, 512, 4096], P(None, 'expert'), may hold values from -6 to 6
- cotangent: bfloat16 [4, 512, 4096], P(None, 'expert'), may hold values from -6 to 6
- gain: float32 [8, 4096], P('section'), may hold values from 0.25 to 1.75
- route: int32 [8, 4, 512, 2], P('section', None, 'expert'), may hold values from 0 to 15, all different within a row; in each aligned block of 32 rows (0 to 31, 32 to 63, ..., all dimensions but the last counted through in order) at most 4 rows name the same one
- gate: float32 [8, 4, 512, 2], P('section', None, 'expert'), may hold values from 0.3 to 1
- w_gate: bfloat16 [8, 16, 4096, 768], P('section', 'expert'), may hold values from -0.09375 to 0.09375
- w_up: bfloat16 [8, 16, 4096, 768], P('section', 'expert'), may hold values from -0.09375 to 0.09375
- w_down: bfloat16 [8, 16, 768, 4096], P('section', 'expert'), may hold values from -0.21875 to 0.21875
Outputs:
- hidden: bfloat16 [8, 4, 512, 4096], P('section', None, 'expert')
- grads: bfloat16 [8, 4, 512, 4096], P('section', None, 'expert')
The draws below stay inside these ranges and needn't reach their ends.
Inputs may be any that keep to these rules, and one draw needn't show every extreme that they name: `route`: each token names 2 different experts. Among the 32 tokens that one device holds of one micro-batch in one section, no expert is named by more than 4 tokens, a bound that some block reaches.
All inputs are finite; a program needn't handle non-finite values.
Results may differ from the reference program's by a relative error of at most 0.03.
Values may be sent and summed in bfloat16 or wider, within the bound.
No kernel may reach another device: no remote copies, remote signals or barrier semaphores. Data moves between devices by JAX's collectives and lax.ppermute only.
A program may use at most 64 MiB of HBM per device.

```python
import math
import jax
import jax.numpy as jnp
import numpy as np
from jax import lax

D = 4096
HID = 768
TOP = 2
MICRO = 4
TOK_MB = 32
EXPERTS = 16
SECTIONS = 8
TOKENS = 512
CAP = 4
N_EXPERT = 16


def level_of(stream_key, extent, split, least, high):
    level = 1.0
    for axis_at, blocks in split:
        heights = jax.random.uniform(jax.random.fold_in(jax.random.fold_in(stream_key, 6), axis_at), (blocks,), jnp.float32, least / len(split), high / len(split))
        level = level * jnp.repeat(jnp.exp(heights), extent[axis_at] // blocks).reshape((-1,) + (1,) * (len(extent) - 1 - axis_at))
    return level


def routed_block(own_key, own, number, rows, amount, top, bound, skew):
    sequence = jax.random.permutation(own_key, amount)
    packed, common = portions_of(amount, rows * top, bound, skew, True), portions_of(amount, rows * top, bound, skew, False)
    places = jnp.arange(amount)

    def named(lengths, rotation):
        used = int((lengths > 0).sum())
        fixed = max(1, used // 4)
        shifted = fixed + (places - fixed + rotation * (used - fixed)) % max(1, amount - fixed)
        return jnp.zeros((amount,), jnp.int32).at[sequence[jnp.where(places < fixed, places, shifted)]].set(jnp.asarray(lengths, jnp.int32))

    lengths = jnp.where(number % 4 == 0, named(packed, number // 4), named(common, number - number // 4 - 1))
    mixed = jax.random.permutation(jax.random.fold_in(own, 3), amount)
    giver, sink = mixed[0:amount // 2 * 2:2], mixed[1:amount // 2 * 2:2]
    slack = jnp.minimum(lengths[giver] - 1, bound - lengths[sink]) // 2
    slack = jnp.where((giver == sequence[0]) | (sink == sequence[0]) | (lengths[sink] == 0), 0, jnp.maximum(slack, 0))
    shifted = jax.random.randint(jax.random.fold_in(own, 4), (amount // 2,), 0, 1 << 20) % (slack + 1)
    lengths = lengths.at[giver].add(-shifted).at[sink].add(shifted)
    members = jnp.searchsorted(jnp.cumsum(lengths), jnp.arange(rows * top), side="right").astype(jnp.int32)
    grid = members.reshape(top, rows).T
    grid = grid[jax.random.permutation(jax.random.fold_in(own, 1), rows)]
    rotation = jax.random.randint(jax.random.fold_in(own, 2), (rows, 1), 0, top)
    return jnp.take_along_axis(grid, (jnp.arange(top)[None, :] + rotation) % top, axis=1)


def portions_of(amount, total, bound, lean, full):
    weights = [(1 << 20) // math.isqrt(standing ** lean) + 1 for standing in range(1, amount + 1)]
    largest = bound if full else min(bound, max(-(-total // amount), total * weights[0] // sum(weights)))
    least = 1 if total - largest >= amount - 1 else 0
    holding, spare = [largest] + [least] * (amount - 1), total - largest - least * (amount - 1)
    while spare > 0:
        movable = [i for i in range(1, amount) if holding[i] < largest] or [i for i in range(1, amount) if holding[i] < bound]
        whole, remaining = sum([weights[i] for i in movable]), spare
        for i in movable:
            extra = min(bound - holding[i], max(1, remaining * weights[i] // whole), spare)
            holding[i] = holding[i] + extra
            spare = spare - extra
    return np.array(holding)


def centred(key, shape, spread, bound, split=(), kind=jnp.bfloat16):
    values = jax.random.normal(key, shape, jnp.float32) * spread
    if len(split) > 0:
        values = level_of(key, shape, split, -0.22, 0.18) * values
    return jnp.clip(values, min=-bound, max=bound).astype(kind)


def setup_inputs(seed: int = 0) -> dict:
    arg_keys = jax.random.split(jax.random.key(seed), 9)
    inputs = centred(arg_keys[0], (MICRO, TOKENS, D), 1.0, 6.0, ((1, 16),))
    cotangent = centred(arg_keys[1], (MICRO, TOKENS, D), 1.0, 6.0, ((1, 16),))
    gain = jnp.clip(1.0 + 0.15 * jax.random.normal(arg_keys[2], (SECTIONS, D), jnp.float32), 0.25, 1.75)
    route_keys = jax.random.split(jax.random.fold_in(arg_keys[3], 1), SECTIONS * MICRO * TOKENS // TOK_MB)
    route_turns = jax.random.permutation(jax.random.fold_in(arg_keys[3], 3), SECTIONS * MICRO * TOKENS // TOK_MB)
    route = jax.vmap(lambda own, number: routed_block(jax.random.fold_in(arg_keys[3], 2), own, number, TOK_MB, EXPERTS, TOP, CAP, 2))(route_keys, route_turns).reshape((SECTIONS, MICRO, TOKENS, TOP))
    gate = jnp.clip(0.3 + 0.7 * jax.random.uniform(arg_keys[4], (SECTIONS, MICRO, TOKENS, TOP), jnp.float32) ** level_of(arg_keys[4], (SECTIONS, MICRO, TOKENS, TOP), ((0, 8), (2, 16)), -0.2, 0.2), 0.3, 1.0)
    w_gate = centred(arg_keys[5], (SECTIONS, EXPERTS, D, HID), D ** -0.5, 0.09375, ((0, 8), (1, 16)))
    w_up = centred(arg_keys[6], (SECTIONS, EXPERTS, D, HID), D ** -0.5, 0.09375, ((0, 8), (1, 16)))
    w_down = centred(arg_keys[7], (SECTIONS, EXPERTS, HID, D), HID ** -0.5, 0.21875, ((0, 8), (1, 16)))
    return {"inputs": inputs, "cotangent": cotangent, "gain": gain, "route": route, "gate": gate, "w_gate": w_gate, "w_up": w_up, "w_down": w_down}


EPS = 1e-06

def block_positions(route):
    blocks = route.reshape(N_EXPERT, TOK_MB * TOP)
    onehot = (blocks[:, :, None] == jnp.arange(EXPERTS, dtype=jnp.int32)[None, None, :]).astype(jnp.int32)
    before = jnp.cumsum(onehot, axis=1) - onehot
    slot = lax.optimization_barrier(jnp.sum(before * onehot, axis=2)).astype(jnp.int32)
    source = jnp.arange(N_EXPERT, dtype=jnp.int32)[:, None]
    return (source * CAP + slot).reshape(route.shape).astype(jnp.int32)

def normalize(tokens, gain):
    values = tokens.astype(jnp.float32)
    scale = lax.rsqrt(lax.optimization_barrier(jnp.mean(values * values, axis=-1, keepdims=True)) + EPS)
    return (values, scale, (values * scale * gain).astype(jnp.bfloat16))

def expert_rows(rows, route, place):
    empty = jnp.zeros((EXPERTS, N_EXPERT * CAP, D), jnp.bfloat16)
    return empty.at[route.reshape(-1), place.reshape(-1)].set(rows.reshape(-1, D))

def forward_experts(buffers, w_gate, w_up, w_down):

    def single(operands):
        rows, weight_gate, weight_up, weight_down = operands
        pre_gate = jnp.dot(rows, weight_gate, preferred_element_type=jnp.float32)
        pre_up = jnp.dot(rows, weight_up, preferred_element_type=jnp.float32)
        product = (pre_gate * jax.nn.sigmoid(pre_gate) * pre_up).astype(jnp.bfloat16)
        output = jnp.dot(product, weight_down, preferred_element_type=jnp.float32).astype(jnp.bfloat16)
        return (output, pre_gate, pre_up)
    return lax.map(single, (buffers, w_gate, w_up, w_down))

def section_forward(tokens, gain, route, gate, w_gate, w_up, w_down):
    values, scale, normed = normalize(tokens, gain)
    place = block_positions(route)
    rows = jnp.broadcast_to(normed[:, None, :], (TOKENS, TOP, D))
    output, pre_gate, pre_up = forward_experts(expert_rows(rows, route, place), w_gate, w_up, w_down)
    picked = output[route, place]
    mixed = values + lax.optimization_barrier(jnp.sum(gate[..., None] * picked.astype(jnp.float32), axis=1))
    return mixed.astype(jnp.bfloat16)

def section_backward(tokens, grad_out, gain, route, gate, w_gate, w_up, w_down):
    values, scale, normed = normalize(tokens, gain)
    place = block_positions(route)
    rows = jnp.broadcast_to(normed[:, None, :], (TOKENS, TOP, D))
    output, pre_gate, pre_up = forward_experts(expert_rows(rows, route, place), w_gate, w_up, w_down)
    scaled = (gate[..., None] * grad_out.astype(jnp.float32)[:, None, :]).astype(jnp.bfloat16)
    grad_rows = expert_rows(scaled, route, place)

    def single(operands):
        grad_block, gate_pre, up_pre, weight_gate, weight_up, weight_down = operands
        d_hidden = jnp.dot(grad_block, weight_down.T, preferred_element_type=jnp.float32)
        sigma = jax.nn.sigmoid(gate_pre)
        d_gate = (d_hidden * up_pre * sigma * (1.0 + gate_pre * (1.0 - sigma))).astype(jnp.bfloat16)
        d_up = (d_hidden * gate_pre * sigma).astype(jnp.bfloat16)
        back = jnp.dot(d_gate, weight_gate.T, preferred_element_type=jnp.float32) + jnp.dot(d_up, weight_up.T, preferred_element_type=jnp.float32)
        return back.astype(jnp.bfloat16)
    back = lax.map(single, (grad_rows, pre_gate, pre_up, w_gate, w_up, w_down))
    d_norm = lax.optimization_barrier(jnp.sum(back[route, place].astype(jnp.float32), axis=1))
    weighted = d_norm * gain
    result = grad_out.astype(jnp.float32) + scale * weighted - values * (scale * scale * scale) * lax.optimization_barrier(jnp.mean(values * weighted, axis=-1, keepdims=True))
    return result.astype(jnp.bfloat16)

def reference(inputs, cotangent, gain, route, gate, w_gate, w_up, w_down):

    def forward(current, per_section):
        gain_s, route_s, gate_s, wg, wu, wd = per_section
        produced = lax.map(lambda item: section_forward(item[0], gain_s, item[1], item[2], wg, wu, wd), (current, route_s, gate_s))
        return (produced, produced)
    _, hidden = lax.scan(forward, inputs, (gain, route, gate, w_gate, w_up, w_down))
    section_inputs = jnp.concatenate([inputs[None], hidden[:-1]], axis=0)

    def backward(grad_now, per_section):
        inputs_s, gain_s, route_s, gate_s, wg, wu, wd = per_section
        produced = lax.map(lambda item: section_backward(item[0], item[1], gain_s, item[2], item[3], wg, wu, wd), (inputs_s, grad_now, route_s, gate_s))
        return (produced, produced)
    _, grads = lax.scan(backward, cotangent, (section_inputs, gain, route, gate, w_gate, w_up, w_down), reverse=True)
    return (hidden, grads)
```

```python
import jax
import jax.numpy as jnp
from jax import lax
from jax.sharding import PartitionSpec as P

EPS = 1e-06


def passed_along(value, axis, steps):
    count = lax.axis_size(axis)
    leading, last = (max(0, -steps), min(count, count - steps))
    return lax.ppermute(value, axis, [(source, source + steps) for source in range(leading, last)])


def slot_places(route, experts, capacity):
    flat = route.reshape(-1)
    onehot = (flat[:, None] == jnp.arange(experts, dtype=jnp.int32)[None, :]).astype(jnp.int32)
    before = jnp.cumsum(onehot, axis=0) - onehot
    slot = jnp.sum(before * onehot, axis=1)
    return (flat * capacity + slot).reshape(route.shape)


def slot_table(places, total_rows):
    grid = jnp.arange(total_rows, dtype=jnp.int32)
    return (places.T[:, :, None] == grid[None, None, :]).astype(jnp.bfloat16)


def normalize(tokens, gain):
    values = tokens.astype(jnp.float32)
    scale = lax.rsqrt(jnp.mean(values * values, axis=-1, keepdims=True) + EPS)
    return (values, scale, (values * scale * gain).astype(jnp.bfloat16))


def pre_products(rows, w_gate, w_up):
    flat = rows.reshape(-1, rows.shape[-1])
    pre_gate = jnp.dot(flat, w_gate, preferred_element_type=jnp.float32)
    pre_up = jnp.dot(flat, w_up, preferred_element_type=jnp.float32)
    inner = rows.shape[:-1] + (w_gate.shape[1],)
    return (pre_gate.reshape(inner), pre_up.reshape(inner))


def expert_forward(rows, w_gate, w_up, w_down):
    pre_gate, pre_up = pre_products(rows, w_gate, w_up)
    width = w_gate.shape[1]
    product = (pre_gate * jax.nn.sigmoid(pre_gate) * pre_up).astype(jnp.bfloat16)
    output = jnp.dot(product.reshape(-1, width), w_down, preferred_element_type=jnp.float32).astype(
        jnp.bfloat16
    )
    return (output.reshape(rows.shape), pre_gate, pre_up)


def contract_last(left, right):
    return lax.dot_general(
        left, right, (((1,), (1,)), ((), ())), preferred_element_type=jnp.float32
    )


def expert_backward(grad_rows, pre_gate, pre_up, w_gate, w_up, w_down):
    shape = grad_rows.shape
    width = w_gate.shape[1]
    flat = grad_rows.reshape(-1, shape[-1])
    gate_pre = pre_gate.reshape(-1, width)
    up_pre = pre_up.reshape(-1, width)
    d_hidden = contract_last(flat, w_down)
    sigma = jax.nn.sigmoid(gate_pre)
    d_gate = (d_hidden * up_pre * sigma * (1.0 + gate_pre * (1.0 - sigma))).astype(jnp.bfloat16)
    d_up = (d_hidden * gate_pre * sigma).astype(jnp.bfloat16)
    back = contract_last(d_gate, w_gate) + contract_last(d_up, w_up)
    return back.astype(jnp.bfloat16).reshape(shape)


def return_rows(rows):
    return lax.all_to_all(rows, "expert", split_axis=0, concat_axis=0, tiled=True)


def local(inputs, cotangent, gain, route, gate, w_gate, w_up, w_down):
    micro, tok, width = inputs.shape
    top = route.shape[-1]
    experts = lax.axis_size("expert")
    capacity = tok * top * 7 // (6 * experts)
    total_rows = experts * capacity
    sections = lax.axis_size("section")
    section = lax.axis_index("section")
    ticks = sections + micro - 1
    gain_row = gain[0]
    weight_gate = w_gate[0, 0]
    weight_up = w_up[0, 0]
    weight_down = w_down[0, 0]
    inner = weight_gate.shape[1]
    routes = route[0]
    gates = gate[0]

    all_places = jax.vmap(lambda r: slot_places(r, experts, capacity))(routes)
    all_tables = jax.vmap(lambda p: slot_table(p, total_rows))(all_places)

    def forward_work(tokens, places, table, gate_now, live):
        values, scale, normed = normalize(tokens, gain_row)
        send = jnp.einsum("ktj,td->jd", table, normed, preferred_element_type=jnp.float32).astype(
            jnp.bfloat16
        )
        send = send.reshape(experts, capacity, width)

        def forward_active(operand):
            return expert_forward(operand, weight_gate, weight_up, weight_down)

        def forward_resting(operand):
            pre_zero = jnp.zeros(operand.shape[:-1] + (inner,), jnp.float32)
            return (jnp.zeros_like(operand), pre_zero, pre_zero)

        output, pre_gate, pre_up = lax.cond(
            live,
            forward_active,
            forward_resting,
            lax.all_to_all(send, "expert", split_axis=0, concat_axis=0, tiled=True),
        )
        back = return_rows(output)
        picked = back.reshape(total_rows, width)[places]
        mixed = values + jnp.sum(gate_now[..., None] * picked.astype(jnp.float32), axis=1)
        return (mixed.astype(jnp.bfloat16), pre_gate, pre_up)

    def forward_tick(carry, tick):
        incoming, outputs, kept_x, kept_gate, kept_up = carry
        offset = tick - section
        live = (offset >= 0) & (offset < micro)
        index = jnp.clip(offset, 0, micro - 1)
        fresh = lax.dynamic_index_in_dim(inputs, index, 0, keepdims=False)
        tokens = jnp.where(section == 0, fresh, incoming)
        places = lax.dynamic_index_in_dim(all_places, index, 0, keepdims=False)
        table = lax.dynamic_index_in_dim(all_tables, index, 0, keepdims=False)
        gate_now = lax.dynamic_index_in_dim(gates, index, 0, keepdims=False)
        mixed, pre_gate, pre_up = forward_work(tokens, places, table, gate_now, live)
        old_out = lax.dynamic_index_in_dim(outputs, index, 0, keepdims=False)
        outputs = lax.dynamic_update_index_in_dim(
            outputs, jnp.where(live, mixed, old_out), index, 0
        )
        old_x = lax.dynamic_index_in_dim(kept_x, index, 0, keepdims=False)
        kept_x = lax.dynamic_update_index_in_dim(kept_x, jnp.where(live, tokens, old_x), index, 0)
        old_gate = lax.dynamic_index_in_dim(kept_gate, index, 0, keepdims=False)
        kept_gate = lax.dynamic_update_index_in_dim(
            kept_gate, jnp.where(live, pre_gate, old_gate), index, 0
        )
        old_up = lax.dynamic_index_in_dim(kept_up, index, 0, keepdims=False)
        kept_up = lax.dynamic_update_index_in_dim(kept_up, jnp.where(live, pre_up, old_up), index, 0)
        incoming = passed_along(mixed, "section", 1)
        return ((incoming, outputs, kept_x, kept_gate, kept_up), None)

    start = (
        jnp.zeros((tok, width), jnp.bfloat16),
        jnp.zeros_like(inputs),
        jnp.zeros_like(inputs),
        jnp.zeros((micro, experts, capacity, inner), jnp.float32),
        jnp.zeros((micro, experts, capacity, inner), jnp.float32),
    )
    finished, _ = lax.scan(forward_tick, start, jnp.arange(ticks, dtype=jnp.int32))
    _, outputs, kept_x, kept_gate, kept_up = finished

    def backward_work(tokens, grad_out, places, table, gate_now, gate_kept, up_kept, live):
        values, scale, normed = normalize(tokens, gain_row)
        scaled = (gate_now[..., None] * grad_out.astype(jnp.float32)[:, None, :]).astype(
            jnp.bfloat16
        )
        grad_send = jnp.einsum(
            "ktj,tkd->jd", table, scaled, preferred_element_type=jnp.float32
        ).astype(jnp.bfloat16)
        grad_send = grad_send.reshape(experts, capacity, width)

        def backward_active(operands):
            rows_grad, gate_again, up_again = operands
            return expert_backward(
                rows_grad, gate_again, up_again, weight_gate, weight_up, weight_down
            )

        def backward_resting(operands):
            return jnp.zeros_like(operands[0])

        computed = lax.cond(
            live,
            backward_active,
            backward_resting,
            (
                lax.all_to_all(grad_send, "expert", split_axis=0, concat_axis=0, tiled=True),
                gate_kept,
                up_kept,
            ),
        )
        back = return_rows(computed)
        d_norm = jnp.sum(back.reshape(total_rows, width)[places].astype(jnp.float32), axis=1)
        weighted = d_norm * gain_row
        result = (
            grad_out.astype(jnp.float32)
            + scale * weighted
            - values * (scale * scale * scale) * jnp.mean(values * weighted, axis=-1, keepdims=True)
        )
        return result.astype(jnp.bfloat16)

    def backward_tick(carry, tick):
        incoming, results = carry
        offset = tick - (sections - 1 - section)
        live = (offset >= 0) & (offset < micro)
        index = jnp.clip(offset, 0, micro - 1)
        fresh = lax.dynamic_index_in_dim(cotangent, index, 0, keepdims=False)
        grad_out = jnp.where(section == sections - 1, fresh, incoming)
        tokens = lax.dynamic_index_in_dim(kept_x, index, 0, keepdims=False)
        places = lax.dynamic_index_in_dim(all_places, index, 0, keepdims=False)
        table = lax.dynamic_index_in_dim(all_tables, index, 0, keepdims=False)
        gate_now = lax.dynamic_index_in_dim(gates, index, 0, keepdims=False)
        gate_kept = lax.dynamic_index_in_dim(kept_gate, index, 0, keepdims=False)
        up_kept = lax.dynamic_index_in_dim(kept_up, index, 0, keepdims=False)
        result = backward_work(
            tokens, grad_out, places, table, gate_now, gate_kept, up_kept, live
        )
        old_result = lax.dynamic_index_in_dim(results, index, 0, keepdims=False)
        results = lax.dynamic_update_index_in_dim(
            results, jnp.where(live, result, old_result), index, 0
        )
        incoming = passed_along(result, "section", -1)
        return ((incoming, results), None)

    done, _ = lax.scan(
        backward_tick,
        (jnp.zeros((tok, width), jnp.bfloat16), jnp.zeros_like(cotangent)),
        jnp.arange(ticks, dtype=jnp.int32),
    )
    results = done[1]
    return (outputs[None], results[None])


def solution(mesh):
    placed = (
        P(None, "expert", None),
        P(None, "expert", None),
        P("section", None),
        P("section", None, "expert", None),
        P("section", None, "expert", None),
        P("section", "expert", None, None),
        P("section", "expert", None, None),
        P("section", "expert", None, None),
    )
    return jax.shard_map(
        local,
        mesh=mesh,
        in_specs=placed,
        out_specs=(P("section", None, "expert", None), P("section", None, "expert", None)),
        check_vma=False,
    )
```

```python
import jax
import jax.numpy as jnp
from jax import lax
from jax.sharding import PartitionSpec as P

EPS = 1e-06


def passed_along(value, axis, steps):
    count = lax.axis_size(axis)
    leading, last = (max(0, -steps), min(count, count - steps))
    return lax.ppermute(value, axis, [(source, source + steps) for source in range(leading, last)])


def slot_places(route, experts, capacity):
    flat = route.reshape(-1)
    onehot = (flat[:, None] == jnp.arange(experts, dtype=jnp.int32)[None, :]).astype(jnp.int32)
    before = jnp.cumsum(onehot, axis=0) - onehot
    slot = jnp.sum(before * onehot, axis=1)
    return (flat * capacity + slot).reshape(route.shape)


def slot_table(places, total_rows):
    grid = jnp.arange(total_rows, dtype=jnp.int32)
    return (places.T[:, :, None] == grid[None, None, :]).astype(jnp.bfloat16)


def normalize(tokens, gain):
    values = tokens.astype(jnp.float32)
    scale = lax.rsqrt(jnp.mean(values * values, axis=-1, keepdims=True) + EPS)
    return (values, scale, (values * scale * gain).astype(jnp.bfloat16))


def pre_products(rows, w_gate, w_up):
    flat = rows.reshape(-1, rows.shape[-1])
    pre_gate = jnp.dot(flat, w_gate, preferred_element_type=jnp.float32)
    pre_up = jnp.dot(flat, w_up, preferred_element_type=jnp.float32)
    inner = rows.shape[:-1] + (w_gate.shape[1],)
    return (pre_gate.reshape(inner), pre_up.reshape(inner))


def expert_forward(rows, w_gate, w_up, w_down):
    pre_gate, pre_up = pre_products(rows, w_gate, w_up)
    width = w_gate.shape[1]
    product = (pre_gate * jax.nn.sigmoid(pre_gate) * pre_up).astype(jnp.bfloat16)
    output = jnp.dot(product.reshape(-1, width), w_down, preferred_element_type=jnp.float32).astype(
        jnp.bfloat16
    )
    return (output.reshape(rows.shape), pre_gate, pre_up)


def contract_last(left, right):
    return lax.dot_general(
        left, right, (((1,), (1,)), ((), ())), preferred_element_type=jnp.float32
    )


def expert_backward(grad_rows, pre_gate, pre_up, w_gate, w_up, w_down):
    shape = grad_rows.shape
    width = w_gate.shape[1]
    flat = grad_rows.reshape(-1, shape[-1])
    gate_pre = pre_gate.reshape(-1, width)
    up_pre = pre_up.reshape(-1, width)
    d_hidden = contract_last(flat, w_down)
    sigma = jax.nn.sigmoid(gate_pre)
    d_gate = (d_hidden * up_pre * sigma * (1.0 + gate_pre * (1.0 - sigma))).astype(jnp.bfloat16)
    d_up = (d_hidden * gate_pre * sigma).astype(jnp.bfloat16)
    back = contract_last(d_gate, w_gate) + contract_last(d_up, w_up)
    return back.astype(jnp.bfloat16).reshape(shape)


def return_rows(rows):
    return lax.all_to_all(rows, "expert", split_axis=0, concat_axis=0, tiled=True)


def local(inputs, cotangent, gain, route, gate, w_gate, w_up, w_down):
    micro, tok, width = inputs.shape
    top = route.shape[-1]
    experts = lax.axis_size("expert")
    capacity = tok * top * 7 // (6 * experts)
    total_rows = experts * capacity
    sections = lax.axis_size("section")
    section = lax.axis_index("section")
    ticks = sections + micro - 1
    gain_row = gain[0]
    weight_gate = w_gate[0, 0]
    weight_up = w_up[0, 0]
    weight_down = w_down[0, 0]
    inner = weight_gate.shape[1]
    routes = route[0]
    gates = gate[0]

    all_places = jax.vmap(lambda r: slot_places(r, experts, capacity))(routes)
    all_tables = jax.vmap(lambda p: slot_table(p, total_rows))(all_places)
    all_weights = jnp.einsum(
        "mktj,mtk->mtj", all_tables.astype(jnp.float32), gates, precision=lax.Precision.HIGHEST
    )
    all_tables4 = all_tables.reshape(micro, top, tok, experts, capacity)

    def forward_work(tokens, table4, weights, live):
        values, scale, normed = normalize(tokens, gain_row)
        send = jnp.einsum(
            "ktec,td->ecd", table4, normed, preferred_element_type=jnp.float32
        ).astype(jnp.bfloat16)

        def forward_active(operand):
            pre_gate, pre_up = pre_products(operand, weight_gate, weight_up)
            product = (pre_gate * jax.nn.sigmoid(pre_gate) * pre_up).astype(jnp.bfloat16)
            output = jnp.einsum(
                "ech,hd->ecd", product, weight_down, preferred_element_type=jnp.float32
            ).astype(jnp.bfloat16)
            return (output, pre_gate, pre_up)

        def forward_resting(operand):
            pre_zero = jnp.zeros(operand.shape[:-1] + (inner,), jnp.float32)
            return (jnp.zeros_like(operand), pre_zero, pre_zero)

        output, pre_gate, pre_up = lax.cond(
            live,
            forward_active,
            forward_resting,
            lax.all_to_all(send, "expert", split_axis=0, concat_axis=0, tiled=True),
        )
        back = return_rows(output).reshape(total_rows, width)
        mixed = values + jnp.dot(
            weights, back.astype(jnp.float32), precision=lax.Precision.HIGHEST
        )
        return (mixed.astype(jnp.bfloat16), pre_gate, pre_up)

    def forward_tick(carry, tick):
        incoming, outputs, kept_x, kept_gate, kept_up = carry
        offset = tick - section
        live = (offset >= 0) & (offset < micro)
        index = jnp.clip(offset, 0, micro - 1)
        slot = jnp.where(live, offset, micro)
        fresh = lax.dynamic_index_in_dim(inputs, index, 0, keepdims=False)
        tokens = jnp.where(section == 0, fresh, incoming)
        table4 = lax.dynamic_index_in_dim(all_tables4, index, 0, keepdims=False)
        weights = lax.dynamic_index_in_dim(all_weights, index, 0, keepdims=False)
        mixed, pre_gate, pre_up = forward_work(tokens, table4, weights, live)
        outputs = lax.dynamic_update_index_in_dim(outputs, mixed, slot, 0)
        kept_x = lax.dynamic_update_index_in_dim(kept_x, tokens, slot, 0)
        kept_gate = lax.dynamic_update_index_in_dim(kept_gate, pre_gate, slot, 0)
        kept_up = lax.dynamic_update_index_in_dim(kept_up, pre_up, slot, 0)
        incoming = passed_along(mixed, "section", 1)
        return ((incoming, outputs, kept_x, kept_gate, kept_up), None)

    spare = (micro + 1,)
    start = (
        jnp.zeros((tok, width), jnp.bfloat16),
        jnp.zeros(spare + inputs.shape[1:], jnp.bfloat16),
        jnp.zeros(spare + inputs.shape[1:], jnp.bfloat16),
        jnp.zeros(spare + (experts, capacity, inner), jnp.float32),
        jnp.zeros(spare + (experts, capacity, inner), jnp.float32),
    )
    finished, _ = lax.scan(forward_tick, start, jnp.arange(ticks, dtype=jnp.int32))
    _, outputs, kept_x, kept_gate, kept_up = finished

    def backward_work(tokens, grad_out, table, table4, gate_now, gate_kept, up_kept, live):
        values, scale, normed = normalize(tokens, gain_row)
        scaled = (gate_now[..., None] * grad_out.astype(jnp.float32)[:, None, :]).astype(
            jnp.bfloat16
        )
        grad_send = jnp.einsum(
            "ktec,tkd->ecd", table4, scaled, preferred_element_type=jnp.float32
        ).astype(jnp.bfloat16)

        def backward_active(operands):
            rows_grad, gate_again, up_again = operands
            return expert_backward(
                rows_grad, gate_again, up_again, weight_gate, weight_up, weight_down
            )

        def backward_resting(operands):
            return jnp.zeros_like(operands[0])

        computed = lax.cond(
            live,
            backward_active,
            backward_resting,
            (
                lax.all_to_all(grad_send, "expert", split_axis=0, concat_axis=0, tiled=True),
                gate_kept,
                up_kept,
            ),
        )
        back = return_rows(computed).reshape(total_rows, width)
        d_norm = jnp.einsum("ktj,jd->td", table, back, preferred_element_type=jnp.float32)
        weighted = d_norm * gain_row
        result = (
            grad_out.astype(jnp.float32)
            + scale * weighted
            - values * (scale * scale * scale) * jnp.mean(values * weighted, axis=-1, keepdims=True)
        )
        return result.astype(jnp.bfloat16)

    def backward_tick(carry, tick):
        incoming, results = carry
        offset = tick - (sections - 1 - section)
        live = (offset >= 0) & (offset < micro)
        index = jnp.clip(offset, 0, micro - 1)
        slot = jnp.where(live, offset, micro)
        fresh = lax.dynamic_index_in_dim(cotangent, index, 0, keepdims=False)
        grad_out = jnp.where(section == sections - 1, fresh, incoming)
        tokens = lax.dynamic_index_in_dim(kept_x, index, 0, keepdims=False)
        table = lax.dynamic_index_in_dim(all_tables, index, 0, keepdims=False)
        table4 = lax.dynamic_index_in_dim(all_tables4, index, 0, keepdims=False)
        gate_now = lax.dynamic_index_in_dim(gates, index, 0, keepdims=False)
        gate_kept = lax.dynamic_index_in_dim(kept_gate, index, 0, keepdims=False)
        up_kept = lax.dynamic_index_in_dim(kept_up, index, 0, keepdims=False)
        result = backward_work(
            tokens, grad_out, table, table4, gate_now, gate_kept, up_kept, live
        )
        results = lax.dynamic_update_index_in_dim(results, result, slot, 0)
        incoming = passed_along(result, "section", -1)
        return ((incoming, results), None)

    done, _ = lax.scan(
        backward_tick,
        (
            jnp.zeros((tok, width), jnp.bfloat16),
            jnp.zeros(spare + cotangent.shape[1:], jnp.bfloat16),
        ),
        jnp.arange(ticks, dtype=jnp.int32),
    )
    results = done[1]
    return (outputs[None, :micro], results[None, :micro])


def solution(mesh):
    placed = (
        P(None, "expert", None),
        P(None, "expert", None),
        P("section", None),
        P("section", None, "expert", None),
        P("section", None, "expert", None),
        P("section", "expert", None, None),
        P("section", "expert", None, None),
        P("section", "expert", None, None),
    )
    return jax.shard_map(
        local,
        mesh=mesh,
        in_specs=placed,
        out_specs=(P("section", None, "expert", None), P("section", None, "expert", None)),
        check_vma=False,
    )
```

```python
import jax
import jax.numpy as jnp
from jax import lax
from jax.experimental import pallas as pl
from jax.experimental.pallas import tpu as pltpu
from jax.sharding import PartitionSpec as P

EPS = 1e-06
HID_BLOCK = 256
NT = (((1,), (1,)), ((), ()))


def _fwd_kernel(rows_ref, wg_ref, wu_ref, wd_ref, out_ref, pg_ref, pu_ref, acc_ref):
    step = pl.program_id(0)

    @pl.when(step == 0)
    def _():
        acc_ref[...] = jnp.zeros_like(acc_ref)

    rows = rows_ref[...]
    pre_gate = jnp.dot(rows, wg_ref[...], preferred_element_type=jnp.float32)
    pre_up = jnp.dot(rows, wu_ref[...], preferred_element_type=jnp.float32)
    pg_ref[...] = pre_gate
    pu_ref[...] = pre_up
    product = (pre_gate * jax.nn.sigmoid(pre_gate) * pre_up).astype(jnp.bfloat16)
    acc_ref[...] += jnp.dot(product, wd_ref[...], preferred_element_type=jnp.float32)

    @pl.when(step == pl.num_programs(0) - 1)
    def _():
        out_ref[...] = acc_ref[...].astype(out_ref.dtype)


def expert_forward_kernel(rows, w_gate, w_up, w_down, interpret=False):
    n, width = rows.shape
    inner = w_gate.shape[1]
    steps = inner // HID_BLOCK
    cost = pl.CostEstimate(
        flops=6 * n * width * inner,
        transcendentals=n * inner,
        bytes_accessed=3 * width * inner * 2 + 2 * n * width * 2 + 2 * n * inner * 4,
    )
    return pl.pallas_call(
        _fwd_kernel,
        grid=(steps,),
        in_specs=[
            pl.BlockSpec((n, width), lambda h: (0, 0)),
            pl.BlockSpec((width, HID_BLOCK), lambda h: (0, h)),
            pl.BlockSpec((width, HID_BLOCK), lambda h: (0, h)),
            pl.BlockSpec((HID_BLOCK, width), lambda h: (h, 0)),
        ],
        out_specs=[
            pl.BlockSpec((n, width), lambda h: (0, 0)),
            pl.BlockSpec((n, HID_BLOCK), lambda h: (0, h)),
            pl.BlockSpec((n, HID_BLOCK), lambda h: (0, h)),
        ],
        out_shape=[
            jax.ShapeDtypeStruct((n, width), jnp.bfloat16),
            jax.ShapeDtypeStruct((n, inner), jnp.float32),
            jax.ShapeDtypeStruct((n, inner), jnp.float32),
        ],
        scratch_shapes=[pltpu.VMEM((n, width), jnp.float32)],
        compiler_params=pltpu.CompilerParams(dimension_semantics=("arbitrary",)),
        cost_estimate=cost,
        interpret=interpret,
    )(rows, w_gate, w_up, w_down)


def _bwd_kernel(grad_ref, pg_ref, pu_ref, wg_ref, wu_ref, wd_ref, back_ref, acc_ref):
    step = pl.program_id(0)

    @pl.when(step == 0)
    def _():
        acc_ref[...] = jnp.zeros_like(acc_ref)

    d_hidden = lax.dot_general(
        grad_ref[...], wd_ref[...], NT, preferred_element_type=jnp.float32
    )
    pre_gate = pg_ref[...]
    pre_up = pu_ref[...]
    sigma = jax.nn.sigmoid(pre_gate)
    d_gate = (d_hidden * pre_up * sigma * (1.0 + pre_gate * (1.0 - sigma))).astype(jnp.bfloat16)
    d_up = (d_hidden * pre_gate * sigma).astype(jnp.bfloat16)
    acc_ref[...] += lax.dot_general(
        d_gate, wg_ref[...], NT, preferred_element_type=jnp.float32
    ) + lax.dot_general(d_up, wu_ref[...], NT, preferred_element_type=jnp.float32)

    @pl.when(step == pl.num_programs(0) - 1)
    def _():
        back_ref[...] = acc_ref[...].astype(back_ref.dtype)


def expert_backward_kernel(grad_rows, pre_gate, pre_up, w_gate, w_up, w_down, interpret=False):
    n, width = grad_rows.shape
    inner = w_gate.shape[1]
    steps = inner // HID_BLOCK
    cost = pl.CostEstimate(
        flops=6 * n * width * inner,
        transcendentals=n * inner,
        bytes_accessed=3 * width * inner * 2 + 2 * n * width * 2 + 2 * n * inner * 4,
    )
    return pl.pallas_call(
        _bwd_kernel,
        grid=(steps,),
        in_specs=[
            pl.BlockSpec((n, width), lambda h: (0, 0)),
            pl.BlockSpec((n, HID_BLOCK), lambda h: (0, h)),
            pl.BlockSpec((n, HID_BLOCK), lambda h: (0, h)),
            pl.BlockSpec((width, HID_BLOCK), lambda h: (0, h)),
            pl.BlockSpec((width, HID_BLOCK), lambda h: (0, h)),
            pl.BlockSpec((HID_BLOCK, width), lambda h: (h, 0)),
        ],
        out_specs=pl.BlockSpec((n, width), lambda h: (0, 0)),
        out_shape=jax.ShapeDtypeStruct((n, width), jnp.bfloat16),
        scratch_shapes=[pltpu.VMEM((n, width), jnp.float32)],
        compiler_params=pltpu.CompilerParams(dimension_semantics=("arbitrary",)),
        cost_estimate=cost,
        interpret=interpret,
    )(grad_rows, pre_gate, pre_up, w_gate, w_up, w_down)


def passed_along(value, axis, steps):
    count = lax.axis_size(axis)
    leading, last = (max(0, -steps), min(count, count - steps))
    return lax.ppermute(value, axis, [(source, source + steps) for source in range(leading, last)])


def slot_places(route, experts, capacity):
    flat = route.reshape(-1)
    onehot = (flat[:, None] == jnp.arange(experts, dtype=jnp.int32)[None, :]).astype(jnp.int32)
    before = jnp.cumsum(onehot, axis=0) - onehot
    slot = jnp.sum(before * onehot, axis=1)
    return (flat * capacity + slot).reshape(route.shape)


def slot_table(places, total_rows):
    grid = jnp.arange(total_rows, dtype=jnp.int32)
    return (places.T[:, :, None] == grid[None, None, :]).astype(jnp.bfloat16)


def normalize(tokens, gain):
    values = tokens.astype(jnp.float32)
    scale = lax.rsqrt(jnp.mean(values * values, axis=-1, keepdims=True) + EPS)
    return (values, scale, (values * scale * gain).astype(jnp.bfloat16))


def pre_products(rows, w_gate, w_up):
    flat = rows.reshape(-1, rows.shape[-1])
    pre_gate = jnp.dot(flat, w_gate, preferred_element_type=jnp.float32)
    pre_up = jnp.dot(flat, w_up, preferred_element_type=jnp.float32)
    inner = rows.shape[:-1] + (w_gate.shape[1],)
    return (pre_gate.reshape(inner), pre_up.reshape(inner))


def expert_forward(rows, w_gate, w_up, w_down):
    pre_gate, pre_up = pre_products(rows, w_gate, w_up)
    width = w_gate.shape[1]
    product = (pre_gate * jax.nn.sigmoid(pre_gate) * pre_up).astype(jnp.bfloat16)
    output = jnp.dot(product.reshape(-1, width), w_down, preferred_element_type=jnp.float32).astype(
        jnp.bfloat16
    )
    return (output.reshape(rows.shape), pre_gate, pre_up)


def contract_last(left, right):
    return lax.dot_general(
        left, right, (((1,), (1,)), ((), ())), preferred_element_type=jnp.float32
    )


def expert_backward(grad_rows, pre_gate, pre_up, w_gate, w_up, w_down):
    shape = grad_rows.shape
    width = w_gate.shape[1]
    flat = grad_rows.reshape(-1, shape[-1])
    gate_pre = pre_gate.reshape(-1, width)
    up_pre = pre_up.reshape(-1, width)
    d_hidden = contract_last(flat, w_down)
    sigma = jax.nn.sigmoid(gate_pre)
    d_gate = (d_hidden * up_pre * sigma * (1.0 + gate_pre * (1.0 - sigma))).astype(jnp.bfloat16)
    d_up = (d_hidden * gate_pre * sigma).astype(jnp.bfloat16)
    back = contract_last(d_gate, w_gate) + contract_last(d_up, w_up)
    return back.astype(jnp.bfloat16).reshape(shape)


def return_rows(rows):
    return lax.all_to_all(rows, "expert", split_axis=0, concat_axis=0, tiled=True)


def local(inputs, cotangent, gain, route, gate, w_gate, w_up, w_down):
    micro, tok, width = inputs.shape
    top = route.shape[-1]
    experts = lax.axis_size("expert")
    capacity = tok * top * 7 // (6 * experts)
    total_rows = experts * capacity
    sections = lax.axis_size("section")
    section = lax.axis_index("section")
    ticks = sections + micro - 1
    gain_row = gain[0]
    weight_gate = w_gate[0, 0]
    weight_up = w_up[0, 0]
    weight_down = w_down[0, 0]
    inner = weight_gate.shape[1]
    routes = route[0]
    gates = gate[0]

    all_places = jax.vmap(lambda r: slot_places(r, experts, capacity))(routes)
    all_tables = jax.vmap(lambda p: slot_table(p, total_rows))(all_places)
    all_weights = jnp.einsum(
        "mktj,mtk->mtj", all_tables.astype(jnp.float32), gates, precision=lax.Precision.HIGHEST
    )
    all_tables4 = all_tables.reshape(micro, top, tok, experts, capacity)

    def forward_work(tokens, table4, weights, live):
        values, scale, normed = normalize(tokens, gain_row)
        send = jnp.einsum(
            "ktec,td->ecd", table4, normed, preferred_element_type=jnp.float32
        ).astype(jnp.bfloat16)

        def forward_active(operand):
            output, pre_gate, pre_up = expert_forward_kernel(
                operand.reshape(total_rows, width), weight_gate, weight_up, weight_down
            )
            return (output.reshape(operand.shape), pre_gate, pre_up)

        def forward_resting(operand):
            pre_zero = jnp.zeros((total_rows, inner), jnp.float32)
            return (jnp.zeros_like(operand), pre_zero, pre_zero)

        output, pre_gate, pre_up = lax.cond(
            live,
            forward_active,
            forward_resting,
            lax.all_to_all(send, "expert", split_axis=0, concat_axis=0, tiled=True),
        )
        back = return_rows(output).reshape(total_rows, width)
        mixed = values + jnp.dot(
            weights, back.astype(jnp.float32), precision=lax.Precision.HIGHEST
        )
        return (mixed.astype(jnp.bfloat16), pre_gate, pre_up)

    def forward_tick(carry, tick):
        incoming, outputs, kept_x, kept_gate, kept_up = carry
        offset = tick - section
        live = (offset >= 0) & (offset < micro)
        index = jnp.clip(offset, 0, micro - 1)
        slot = jnp.where(live, offset, micro)
        fresh = lax.dynamic_index_in_dim(inputs, index, 0, keepdims=False)
        tokens = jnp.where(section == 0, fresh, incoming)
        table4 = lax.dynamic_index_in_dim(all_tables4, index, 0, keepdims=False)
        weights = lax.dynamic_index_in_dim(all_weights, index, 0, keepdims=False)
        mixed, pre_gate, pre_up = forward_work(tokens, table4, weights, live)
        outputs = lax.dynamic_update_index_in_dim(outputs, mixed, slot, 0)
        kept_x = lax.dynamic_update_index_in_dim(kept_x, tokens, slot, 0)
        kept_gate = lax.dynamic_update_index_in_dim(kept_gate, pre_gate, slot, 0)
        kept_up = lax.dynamic_update_index_in_dim(kept_up, pre_up, slot, 0)
        incoming = passed_along(mixed, "section", 1)
        return ((incoming, outputs, kept_x, kept_gate, kept_up), None)

    spare = (micro + 1,)
    start = (
        jnp.zeros((tok, width), jnp.bfloat16),
        jnp.zeros(spare + inputs.shape[1:], jnp.bfloat16),
        jnp.zeros(spare + inputs.shape[1:], jnp.bfloat16),
        jnp.zeros(spare + (total_rows, inner), jnp.float32),
        jnp.zeros(spare + (total_rows, inner), jnp.float32),
    )
    finished, _ = lax.scan(forward_tick, start, jnp.arange(ticks, dtype=jnp.int32))
    _, outputs, kept_x, kept_gate, kept_up = finished

    def backward_work(tokens, grad_out, table, table4, gate_now, gate_kept, up_kept, live):
        values, scale, normed = normalize(tokens, gain_row)
        scaled = (gate_now[..., None] * grad_out.astype(jnp.float32)[:, None, :]).astype(
            jnp.bfloat16
        )
        grad_send = jnp.einsum(
            "ktec,tkd->ecd", table4, scaled, preferred_element_type=jnp.float32
        ).astype(jnp.bfloat16)

        def backward_active(operands):
            rows_grad, gate_again, up_again = operands
            back = expert_backward_kernel(
                rows_grad.reshape(total_rows, width),
                gate_again,
                up_again,
                weight_gate,
                weight_up,
                weight_down,
            )
            return back.reshape(rows_grad.shape)

        def backward_resting(operands):
            return jnp.zeros_like(operands[0])

        computed = lax.cond(
            live,
            backward_active,
            backward_resting,
            (
                lax.all_to_all(grad_send, "expert", split_axis=0, concat_axis=0, tiled=True),
                gate_kept,
                up_kept,
            ),
        )
        back = return_rows(computed).reshape(total_rows, width)
        d_norm = jnp.einsum("ktj,jd->td", table, back, preferred_element_type=jnp.float32)
        weighted = d_norm * gain_row
        result = (
            grad_out.astype(jnp.float32)
            + scale * weighted
            - values * (scale * scale * scale) * jnp.mean(values * weighted, axis=-1, keepdims=True)
        )
        return result.astype(jnp.bfloat16)

    def backward_tick(carry, tick):
        incoming, results = carry
        offset = tick - (sections - 1 - section)
        live = (offset >= 0) & (offset < micro)
        index = jnp.clip(offset, 0, micro - 1)
        slot = jnp.where(live, offset, micro)
        fresh = lax.dynamic_index_in_dim(cotangent, index, 0, keepdims=False)
        grad_out = jnp.where(section == sections - 1, fresh, incoming)
        tokens = lax.dynamic_index_in_dim(kept_x, index, 0, keepdims=False)
        table = lax.dynamic_index_in_dim(all_tables, index, 0, keepdims=False)
        table4 = lax.dynamic_index_in_dim(all_tables4, index, 0, keepdims=False)
        gate_now = lax.dynamic_index_in_dim(gates, index, 0, keepdims=False)
        gate_kept = lax.dynamic_index_in_dim(kept_gate, index, 0, keepdims=False)
        up_kept = lax.dynamic_index_in_dim(kept_up, index, 0, keepdims=False)
        result = backward_work(
            tokens, grad_out, table, table4, gate_now, gate_kept, up_kept, live
        )
        results = lax.dynamic_update_index_in_dim(results, result, slot, 0)
        incoming = passed_along(result, "section", -1)
        return ((incoming, results), None)

    done, _ = lax.scan(
        backward_tick,
        (
            jnp.zeros((tok, width), jnp.bfloat16),
            jnp.zeros(spare + cotangent.shape[1:], jnp.bfloat16),
        ),
        jnp.arange(ticks, dtype=jnp.int32),
    )
    results = done[1]
    return (outputs[None, :micro], results[None, :micro])


def solution(mesh):
    placed = (
        P(None, "expert", None),
        P(None, "expert", None),
        P("section", None),
        P("section", None, "expert", None),
        P("section", None, "expert", None),
        P("section", "expert", None, None),
        P("section", "expert", None, None),
        P("section", "expert", None, None),
    )
    return jax.shard_map(
        local,
        mesh=mesh,
        in_specs=placed,
        out_specs=(P("section", None, "expert", None), P("section", None, "expert", None)),
        check_vma=False,
    )
```

```python
import jax
import jax.numpy as jnp
from jax import lax
from jax.sharding import PartitionSpec as P

EPS = 1e-06


def passed_along(value, axis, steps):
    count = lax.axis_size(axis)
    leading, last = (max(0, -steps), min(count, count - steps))
    return lax.ppermute(value, axis, [(source, source + steps) for source in range(leading, last)])


def slot_places(route, experts, capacity):
    flat = route.reshape(-1)
    onehot = (flat[:, None] == jnp.arange(experts, dtype=jnp.int32)[None, :]).astype(jnp.int32)
    before = jnp.cumsum(onehot, axis=0) - onehot
    slot = jnp.sum(before * onehot, axis=1)
    return (flat * capacity + slot).reshape(route.shape)


def slot_table(places, total_rows):
    grid = jnp.arange(total_rows, dtype=jnp.int32)
    return (places.T[:, :, None] == grid[None, None, :]).astype(jnp.bfloat16)


def normalize(tokens, gain):
    values = tokens.astype(jnp.float32)
    scale = lax.rsqrt(jnp.mean(values * values, axis=-1, keepdims=True) + EPS)
    return (values, scale, (values * scale * gain).astype(jnp.bfloat16))


def pre_products(rows, w_gate, w_up):
    flat = rows.reshape(-1, rows.shape[-1])
    pre_gate = jnp.dot(flat, w_gate, preferred_element_type=jnp.float32)
    pre_up = jnp.dot(flat, w_up, preferred_element_type=jnp.float32)
    inner = rows.shape[:-1] + (w_gate.shape[1],)
    return (pre_gate.reshape(inner), pre_up.reshape(inner))


def expert_forward(rows, w_gate, w_up, w_down):
    pre_gate, pre_up = pre_products(rows, w_gate, w_up)
    width = w_gate.shape[1]
    product = (pre_gate * jax.nn.sigmoid(pre_gate) * pre_up).astype(jnp.bfloat16)
    output = jnp.dot(product.reshape(-1, width), w_down, preferred_element_type=jnp.float32).astype(
        jnp.bfloat16
    )
    return (output.reshape(rows.shape), pre_gate, pre_up)


def contract_last(left, right):
    return lax.dot_general(
        left, right, (((1,), (1,)), ((), ())), preferred_element_type=jnp.float32
    )


def expert_backward(grad_rows, pre_gate, pre_up, w_gate, w_up, w_down):
    shape = grad_rows.shape
    width = w_gate.shape[1]
    flat = grad_rows.reshape(-1, shape[-1])
    gate_pre = pre_gate.reshape(-1, width)
    up_pre = pre_up.reshape(-1, width)
    d_hidden = contract_last(flat, w_down)
    sigma = jax.nn.sigmoid(gate_pre)
    d_gate = (d_hidden * up_pre * sigma * (1.0 + gate_pre * (1.0 - sigma))).astype(jnp.bfloat16)
    d_up = (d_hidden * gate_pre * sigma).astype(jnp.bfloat16)
    back = contract_last(d_gate, w_gate) + contract_last(d_up, w_up)
    return back.astype(jnp.bfloat16).reshape(shape)


def return_rows(rows):
    return lax.all_to_all(rows, "expert", split_axis=0, concat_axis=0, tiled=True)


def local(inputs, cotangent, gain, route, gate, w_gate, w_up, w_down):
    micro, tok, width = inputs.shape
    top = route.shape[-1]
    experts = lax.axis_size("expert")
    capacity = tok * top * 7 // (6 * experts)
    total_rows = experts * capacity
    sections = lax.axis_size("section")
    section = lax.axis_index("section")
    ticks = sections + micro - 1
    gain_row = gain[0]
    weight_gate = w_gate[0, 0]
    weight_up = w_up[0, 0]
    weight_down = w_down[0, 0]
    inner = weight_gate.shape[1]
    routes = route[0]
    gates = gate[0]

    all_places = jax.vmap(lambda r: slot_places(r, experts, capacity))(routes)
    all_tables = jax.vmap(lambda p: slot_table(p, total_rows))(all_places)
    all_weights = jnp.einsum(
        "mktj,mtk->mtj", all_tables.astype(jnp.float32), gates, precision=lax.Precision.HIGHEST
    )
    all_tables4 = all_tables.reshape(micro, top, tok, experts, capacity)

    def forward_work(tokens, table4, weights, live):
        values, scale, normed = normalize(tokens, gain_row)
        send = jnp.einsum(
            "ktec,td->ecd", table4, normed, preferred_element_type=jnp.float32
        ).astype(jnp.bfloat16)

        def forward_active(operand):
            pre_gate, pre_up = pre_products(
                operand.reshape(total_rows, width), weight_gate, weight_up
            )
            product = (pre_gate * jax.nn.sigmoid(pre_gate) * pre_up).astype(jnp.bfloat16)
            output = jnp.einsum(
                "ech,hd->ecd",
                product.reshape(experts, capacity, inner),
                weight_down,
                preferred_element_type=jnp.float32,
            ).astype(jnp.bfloat16)
            return (output, pre_gate, pre_up)

        def forward_resting(operand):
            pre_zero = jnp.zeros((total_rows, inner), jnp.float32)
            return (jnp.zeros_like(operand), pre_zero, pre_zero)

        output, pre_gate, pre_up = lax.cond(
            live,
            forward_active,
            forward_resting,
            lax.all_to_all(send, "expert", split_axis=0, concat_axis=0, tiled=True),
        )
        back = return_rows(output).reshape(total_rows, width)
        mixed = values + jnp.dot(
            weights, back.astype(jnp.float32), precision=lax.Precision.HIGHEST
        )
        return (mixed.astype(jnp.bfloat16), pre_gate, pre_up)

    def forward_tick(carry, tick):
        incoming, outputs, kept_x, kept_gate, kept_up = carry
        offset = tick - section
        live = (offset >= 0) & (offset < micro)
        index = jnp.clip(offset, 0, micro - 1)
        slot = jnp.where(live, offset, micro)
        fresh = lax.dynamic_index_in_dim(inputs, index, 0, keepdims=False)
        tokens = jnp.where(section == 0, fresh, incoming)
        table4 = lax.dynamic_index_in_dim(all_tables4, index, 0, keepdims=False)
        weights = lax.dynamic_index_in_dim(all_weights, index, 0, keepdims=False)
        mixed, pre_gate, pre_up = forward_work(tokens, table4, weights, live)
        outputs = lax.dynamic_update_index_in_dim(outputs, mixed, slot, 0)
        kept_x = lax.dynamic_update_index_in_dim(kept_x, tokens, slot, 0)
        kept_gate = lax.dynamic_update_index_in_dim(kept_gate, pre_gate, slot, 0)
        kept_up = lax.dynamic_update_index_in_dim(kept_up, pre_up, slot, 0)
        incoming = passed_along(mixed, "section", 1)
        return ((incoming, outputs, kept_x, kept_gate, kept_up), None)

    spare = (micro + 1,)
    start = (
        jnp.zeros((tok, width), jnp.bfloat16),
        jnp.zeros(spare + inputs.shape[1:], jnp.bfloat16),
        jnp.zeros(spare + inputs.shape[1:], jnp.bfloat16),
        jnp.zeros(spare + (total_rows, inner), jnp.float32),
        jnp.zeros(spare + (total_rows, inner), jnp.float32),
    )
    finished, _ = lax.scan(forward_tick, start, jnp.arange(ticks, dtype=jnp.int32))
    _, outputs, kept_x, kept_gate, kept_up = finished
    down_across = lax.optimization_barrier(jnp.transpose(weight_down))

    def backward_work(tokens, grad_out, table, table4, gate_now, gate_kept, up_kept, live):
        values, scale, normed = normalize(tokens, gain_row)
        scaled = (gate_now[..., None] * grad_out.astype(jnp.float32)[:, None, :]).astype(
            jnp.bfloat16
        )
        grad_send = jnp.einsum(
            "ktec,tkd->ecd", table4, scaled, preferred_element_type=jnp.float32
        ).astype(jnp.bfloat16)

        def backward_active(operands):
            rows_grad, gate_pre, up_pre = operands
            d_hidden = jnp.dot(
                rows_grad.reshape(total_rows, width),
                down_across,
                preferred_element_type=jnp.float32,
            )
            sigma = jax.nn.sigmoid(gate_pre)
            d_gate = (d_hidden * up_pre * sigma * (1.0 + gate_pre * (1.0 - sigma))).astype(
                jnp.bfloat16
            )
            d_up = (d_hidden * gate_pre * sigma).astype(jnp.bfloat16)
            shape3 = (experts, capacity, inner)
            back = jnp.einsum(
                "ech,dh->ecd",
                d_gate.reshape(shape3),
                weight_gate,
                preferred_element_type=jnp.float32,
            ) + jnp.einsum(
                "ech,dh->ecd", d_up.reshape(shape3), weight_up, preferred_element_type=jnp.float32
            )
            return back.astype(jnp.bfloat16)

        def backward_resting(operands):
            return jnp.zeros_like(operands[0])

        computed = lax.cond(
            live,
            backward_active,
            backward_resting,
            (
                lax.all_to_all(grad_send, "expert", split_axis=0, concat_axis=0, tiled=True),
                gate_kept,
                up_kept,
            ),
        )
        back = return_rows(computed).reshape(total_rows, width)
        d_norm = jnp.einsum("ktj,jd->td", table, back, preferred_element_type=jnp.float32)
        weighted = d_norm * gain_row
        result = (
            grad_out.astype(jnp.float32)
            + scale * weighted
            - values * (scale * scale * scale) * jnp.mean(values * weighted, axis=-1, keepdims=True)
        )
        return result.astype(jnp.bfloat16)

    def backward_tick(carry, tick):
        incoming, results = carry
        offset = tick - (sections - 1 - section)
        live = (offset >= 0) & (offset < micro)
        index = jnp.clip(offset, 0, micro - 1)
        slot = jnp.where(live, offset, micro)
        fresh = lax.dynamic_index_in_dim(cotangent, index, 0, keepdims=False)
        grad_out = jnp.where(section == sections - 1, fresh, incoming)
        tokens = lax.dynamic_index_in_dim(kept_x, index, 0, keepdims=False)
        table = lax.dynamic_index_in_dim(all_tables, index, 0, keepdims=False)
        table4 = lax.dynamic_index_in_dim(all_tables4, index, 0, keepdims=False)
        gate_now = lax.dynamic_index_in_dim(gates, index, 0, keepdims=False)
        gate_kept = lax.dynamic_index_in_dim(kept_gate, index, 0, keepdims=False)
        up_kept = lax.dynamic_index_in_dim(kept_up, index, 0, keepdims=False)
        result = backward_work(
            tokens, grad_out, table, table4, gate_now, gate_kept, up_kept, live
        )
        results = lax.dynamic_update_index_in_dim(results, result, slot, 0)
        incoming = passed_along(result, "section", -1)
        return ((incoming, results), None)

    done, _ = lax.scan(
        backward_tick,
        (
            jnp.zeros((tok, width), jnp.bfloat16),
            jnp.zeros(spare + cotangent.shape[1:], jnp.bfloat16),
        ),
        jnp.arange(ticks, dtype=jnp.int32),
    )
    results = done[1]
    return (outputs[None, :micro], results[None, :micro])


def solution(mesh):
    placed = (
        P(None, "expert", None),
        P(None, "expert", None),
        P("section", None),
        P("section", None, "expert", None),
        P("section", None, "expert", None),
        P("section", "expert", None, None),
        P("section", "expert", None, None),
        P("section", "expert", None, None),
    )
    return jax.shard_map(
        local,
        mesh=mesh,
        in_specs=placed,
        out_specs=(P("section", None, "expert", None), P("section", None, "expert", None)),
        check_vma=False,
    )
```

```python
import jax
import jax.numpy as jnp
from jax import lax
from jax.sharding import PartitionSpec as P

EPS = 1e-06


def passed_along(value, axis, steps):
    count = lax.axis_size(axis)
    leading, last = (max(0, -steps), min(count, count - steps))
    return lax.ppermute(value, axis, [(source, source + steps) for source in range(leading, last)])


def slot_places(route, experts, capacity):
    flat = route.reshape(-1)
    onehot = (flat[:, None] == jnp.arange(experts, dtype=jnp.int32)[None, :]).astype(jnp.int32)
    before = jnp.cumsum(onehot, axis=0) - onehot
    slot = jnp.sum(before * onehot, axis=1)
    return (flat * capacity + slot).reshape(route.shape)


def slot_table(places, total_rows):
    grid = jnp.arange(total_rows, dtype=jnp.int32)
    return (places.T[:, :, None] == grid[None, None, :]).astype(jnp.bfloat16)


def normalize(tokens, gain):
    values = tokens.astype(jnp.float32)
    scale = lax.rsqrt(jnp.mean(values * values, axis=-1, keepdims=True) + EPS)
    return (values, scale, (values * scale * gain).astype(jnp.bfloat16))


def pre_products(rows, w_gate, w_up):
    flat = rows.reshape(-1, rows.shape[-1])
    pre_gate = jnp.dot(flat, w_gate, preferred_element_type=jnp.float32)
    pre_up = jnp.dot(flat, w_up, preferred_element_type=jnp.float32)
    inner = rows.shape[:-1] + (w_gate.shape[1],)
    return (pre_gate.reshape(inner), pre_up.reshape(inner))


def expert_forward(rows, w_gate, w_up, w_down):
    pre_gate, pre_up = pre_products(rows, w_gate, w_up)
    width = w_gate.shape[1]
    product = (pre_gate * jax.nn.sigmoid(pre_gate) * pre_up).astype(jnp.bfloat16)
    output = jnp.dot(product.reshape(-1, width), w_down, preferred_element_type=jnp.float32).astype(
        jnp.bfloat16
    )
    return (output.reshape(rows.shape), pre_gate, pre_up)


def contract_last(left, right):
    return lax.dot_general(
        left, right, (((1,), (1,)), ((), ())), preferred_element_type=jnp.float32
    )


def expert_backward(grad_rows, pre_gate, pre_up, w_gate, w_up, w_down):
    shape = grad_rows.shape
    width = w_gate.shape[1]
    flat = grad_rows.reshape(-1, shape[-1])
    gate_pre = pre_gate.reshape(-1, width)
    up_pre = pre_up.reshape(-1, width)
    d_hidden = contract_last(flat, w_down)
    sigma = jax.nn.sigmoid(gate_pre)
    d_gate = (d_hidden * up_pre * sigma * (1.0 + gate_pre * (1.0 - sigma))).astype(jnp.bfloat16)
    d_up = (d_hidden * gate_pre * sigma).astype(jnp.bfloat16)
    back = contract_last(d_gate, w_gate) + contract_last(d_up, w_up)
    return back.astype(jnp.bfloat16).reshape(shape)


def return_rows(rows):
    return lax.all_to_all(rows, "expert", split_axis=0, concat_axis=0, tiled=True)


def local(inputs, cotangent, gain, route, gate, w_gate, w_up, w_down):
    micro, tok, width = inputs.shape
    top = route.shape[-1]
    experts = lax.axis_size("expert")
    capacity = tok * top * 7 // (6 * experts)
    total_rows = experts * capacity
    sections = lax.axis_size("section")
    section = lax.axis_index("section")
    ticks = sections + micro - 1
    gain_row = gain[0]
    weight_gate = w_gate[0, 0]
    weight_up = w_up[0, 0]
    weight_down = w_down[0, 0]
    inner = weight_gate.shape[1]
    routes = route[0]
    gates = gate[0]

    all_places = jax.vmap(lambda r: slot_places(r, experts, capacity))(routes)
    all_tables = jax.vmap(lambda p: slot_table(p, total_rows))(all_places)
    all_weights = jnp.einsum(
        "mktj,mtk->mtj", all_tables.astype(jnp.float32), gates, precision=lax.Precision.HIGHEST
    )
    all_tables4 = all_tables.reshape(micro, top, tok, experts, capacity)

    def forward_work(tokens, table4, weights, live):
        values, scale, normed = normalize(tokens, gain_row)
        send = jnp.einsum(
            "ktec,td->ecd", table4, normed, preferred_element_type=jnp.float32
        ).astype(jnp.bfloat16)

        def forward_active(operand):
            pre_gate, pre_up = pre_products(operand, weight_gate, weight_up)
            product = (pre_gate * jax.nn.sigmoid(pre_gate) * pre_up).astype(jnp.bfloat16)
            output = jnp.einsum(
                "ech,hd->ecd", product, weight_down, preferred_element_type=jnp.float32
            ).astype(jnp.bfloat16)
            return (output, pre_gate, pre_up)

        def forward_resting(operand):
            pre_zero = jnp.zeros(operand.shape[:-1] + (inner,), jnp.float32)
            return (jnp.zeros_like(operand), pre_zero, pre_zero)

        output, pre_gate, pre_up = lax.cond(
            live,
            forward_active,
            forward_resting,
            lax.all_to_all(send, "expert", split_axis=0, concat_axis=0, tiled=True),
        )
        back = return_rows(output).reshape(total_rows, width)
        mixed = values + jnp.dot(
            weights, back.astype(jnp.float32), precision=lax.Precision.HIGHEST
        )
        return (mixed.astype(jnp.bfloat16), pre_gate, pre_up)

    def forward_tick(carry, tick):
        incoming, outputs, kept_x, kept_gate, kept_up = carry
        offset = tick - section
        live = (offset >= 0) & (offset < micro)
        index = jnp.clip(offset, 0, micro - 1)
        slot = jnp.where(live, offset, micro)
        fresh = lax.dynamic_index_in_dim(inputs, index, 0, keepdims=False)
        tokens = jnp.where(section == 0, fresh, incoming)
        table4 = lax.dynamic_index_in_dim(all_tables4, index, 0, keepdims=False)
        weights = lax.dynamic_index_in_dim(all_weights, index, 0, keepdims=False)
        mixed, pre_gate, pre_up = forward_work(tokens, table4, weights, live)
        outputs = lax.dynamic_update_index_in_dim(outputs, mixed, slot, 0)
        kept_x = lax.dynamic_update_index_in_dim(kept_x, tokens, slot, 0)
        kept_gate = lax.dynamic_update_index_in_dim(
            kept_gate, pre_gate.reshape(total_rows, inner), slot, 0
        )
        kept_up = lax.dynamic_update_index_in_dim(
            kept_up, pre_up.reshape(total_rows, inner), slot, 0
        )
        incoming = passed_along(mixed, "section", 1)
        return ((incoming, outputs, kept_x, kept_gate, kept_up), None)

    spare = (micro + 1,)
    start = (
        jnp.zeros((tok, width), jnp.bfloat16),
        jnp.zeros(spare + inputs.shape[1:], jnp.bfloat16),
        jnp.zeros(spare + inputs.shape[1:], jnp.bfloat16),
        jnp.zeros(spare + (total_rows, inner), jnp.float32),
        jnp.zeros(spare + (total_rows, inner), jnp.float32),
    )
    finished, _ = lax.scan(forward_tick, start, jnp.arange(ticks, dtype=jnp.int32))
    _, outputs, kept_x, kept_gate, kept_up = finished
    down_across = lax.optimization_barrier(jnp.transpose(weight_down))

    def backward_work(tokens, grad_out, table, table4, gate_now, gate_kept, up_kept, live):
        values, scale, normed = normalize(tokens, gain_row)
        scaled = (gate_now[..., None] * grad_out.astype(jnp.float32)[:, None, :]).astype(
            jnp.bfloat16
        )
        grad_send = jnp.einsum(
            "ktec,tkd->ecd", table4, scaled, preferred_element_type=jnp.float32
        ).astype(jnp.bfloat16)

        def backward_active(operands):
            rows_grad, gate_pre, up_pre = operands
            d_hidden = jnp.dot(
                rows_grad.reshape(total_rows, width),
                down_across,
                preferred_element_type=jnp.float32,
            )
            sigma = jax.nn.sigmoid(gate_pre)
            d_gate = (d_hidden * up_pre * sigma * (1.0 + gate_pre * (1.0 - sigma))).astype(
                jnp.bfloat16
            )
            d_up = (d_hidden * gate_pre * sigma).astype(jnp.bfloat16)
            back = contract_last(d_gate, weight_gate) + contract_last(d_up, weight_up)
            return back.astype(jnp.bfloat16).reshape(rows_grad.shape)

        def backward_resting(operands):
            return jnp.zeros_like(operands[0])

        computed = lax.cond(
            live,
            backward_active,
            backward_resting,
            (
                lax.all_to_all(grad_send, "expert", split_axis=0, concat_axis=0, tiled=True),
                gate_kept,
                up_kept,
            ),
        )
        back = return_rows(computed).reshape(total_rows, width)
        d_norm = jnp.einsum("ktj,jd->td", table, back, preferred_element_type=jnp.float32)
        weighted = d_norm * gain_row
        result = (
            grad_out.astype(jnp.float32)
            + scale * weighted
            - values * (scale * scale * scale) * jnp.mean(values * weighted, axis=-1, keepdims=True)
        )
        return result.astype(jnp.bfloat16)

    def backward_tick(carry, tick):
        incoming, results = carry
        offset = tick - (sections - 1 - section)
        live = (offset >= 0) & (offset < micro)
        index = jnp.clip(offset, 0, micro - 1)
        slot = jnp.where(live, offset, micro)
        fresh = lax.dynamic_index_in_dim(cotangent, index, 0, keepdims=False)
        grad_out = jnp.where(section == sections - 1, fresh, incoming)
        tokens = lax.dynamic_index_in_dim(kept_x, index, 0, keepdims=False)
        table = lax.dynamic_index_in_dim(all_tables, index, 0, keepdims=False)
        table4 = lax.dynamic_index_in_dim(all_tables4, index, 0, keepdims=False)
        gate_now = lax.dynamic_index_in_dim(gates, index, 0, keepdims=False)
        gate_kept = lax.dynamic_index_in_dim(kept_gate, index, 0, keepdims=False)
        up_kept = lax.dynamic_index_in_dim(kept_up, index, 0, keepdims=False)
        result = backward_work(
            tokens, grad_out, table, table4, gate_now, gate_kept, up_kept, live
        )
        results = lax.dynamic_update_index_in_dim(results, result, slot, 0)
        incoming = passed_along(result, "section", -1)
        return ((incoming, results), None)

    done, _ = lax.scan(
        backward_tick,
        (
            jnp.zeros((tok, width), jnp.bfloat16),
            jnp.zeros(spare + cotangent.shape[1:], jnp.bfloat16),
        ),
        jnp.arange(ticks, dtype=jnp.int32),
    )
    results = done[1]
    return (outputs[None, :micro], results[None, :micro])


def solution(mesh):
    placed = (
        P(None, "expert", None),
        P(None, "expert", None),
        P("section", None),
        P("section", None, "expert", None),
        P("section", None, "expert", None),
        P("section", "expert", None, None),
        P("section", "expert", None, None),
        P("section", "expert", None, None),
    )
    return jax.shard_map(
        local,
        mesh=mesh,
        in_specs=placed,
        out_specs=(P("section", None, "expert", None), P("section", None, "expert", None)),
        check_vma=False,
    )
```

```python
import jax
import jax.numpy as jnp
from jax import lax
from jax.sharding import PartitionSpec as P

EPS = 1e-06


def passed_along(value, axis, steps):
    count = lax.axis_size(axis)
    leading, last = (max(0, -steps), min(count, count - steps))
    return lax.ppermute(value, axis, [(source, source + steps) for source in range(leading, last)])


def slot_places(route, experts, capacity):
    flat = route.reshape(-1)
    onehot = (flat[:, None] == jnp.arange(experts, dtype=jnp.int32)[None, :]).astype(jnp.int32)
    before = jnp.cumsum(onehot, axis=0) - onehot
    slot = jnp.sum(before * onehot, axis=1)
    return (flat * capacity + slot).reshape(route.shape)


def slot_table(places, total_rows):
    grid = jnp.arange(total_rows, dtype=jnp.int32)
    return (places.T[:, :, None] == grid[None, None, :]).astype(jnp.bfloat16)


def normalize(tokens, gain):
    values = tokens.astype(jnp.float32)
    scale = lax.rsqrt(jnp.mean(values * values, axis=-1, keepdims=True) + EPS)
    return (values, scale, (values * scale * gain).astype(jnp.bfloat16))


def pre_products(rows, w_gate, w_up):
    flat = rows.reshape(-1, rows.shape[-1])
    pre_gate = jnp.dot(flat, w_gate, preferred_element_type=jnp.float32)
    pre_up = jnp.dot(flat, w_up, preferred_element_type=jnp.float32)
    inner = rows.shape[:-1] + (w_gate.shape[1],)
    return (pre_gate.reshape(inner), pre_up.reshape(inner))


def expert_forward(rows, w_gate, w_up, w_down):
    pre_gate, pre_up = pre_products(rows, w_gate, w_up)
    width = w_gate.shape[1]
    product = (pre_gate * jax.nn.sigmoid(pre_gate) * pre_up).astype(jnp.bfloat16)
    output = jnp.dot(product.reshape(-1, width), w_down, preferred_element_type=jnp.float32).astype(
        jnp.bfloat16
    )
    return (output.reshape(rows.shape), pre_gate, pre_up)


def contract_last(left, right):
    return lax.dot_general(
        left, right, (((1,), (1,)), ((), ())), preferred_element_type=jnp.float32
    )


def expert_backward(grad_rows, pre_gate, pre_up, w_gate, w_up, w_down):
    shape = grad_rows.shape
    width = w_gate.shape[1]
    flat = grad_rows.reshape(-1, shape[-1])
    gate_pre = pre_gate.reshape(-1, width)
    up_pre = pre_up.reshape(-1, width)
    d_hidden = contract_last(flat, w_down)
    sigma = jax.nn.sigmoid(gate_pre)
    d_gate = (d_hidden * up_pre * sigma * (1.0 + gate_pre * (1.0 - sigma))).astype(jnp.bfloat16)
    d_up = (d_hidden * gate_pre * sigma).astype(jnp.bfloat16)
    back = contract_last(d_gate, w_gate) + contract_last(d_up, w_up)
    return back.astype(jnp.bfloat16).reshape(shape)


def return_rows(rows):
    return lax.all_to_all(rows, "expert", split_axis=0, concat_axis=0, tiled=True)


def local(inputs, cotangent, gain, route, gate, w_gate, w_up, w_down):
    micro, tok, width = inputs.shape
    top = route.shape[-1]
    experts = lax.axis_size("expert")
    capacity = tok * top * 7 // (6 * experts)
    total_rows = experts * capacity
    sections = lax.axis_size("section")
    section = lax.axis_index("section")
    ticks = sections + micro - 1
    gain_row = gain[0]
    weight_gate = w_gate[0, 0]
    weight_up = w_up[0, 0]
    weight_down = w_down[0, 0]
    inner = weight_gate.shape[1]
    routes = route[0]
    gates = gate[0]

    all_places = jax.vmap(lambda r: slot_places(r, experts, capacity))(routes)
    all_tables = jax.vmap(lambda p: slot_table(p, total_rows))(all_places)
    all_weights = jnp.einsum(
        "mktj,mtk->mtj", all_tables.astype(jnp.float32), gates, precision=lax.Precision.HIGHEST
    )
    all_tables4 = all_tables.reshape(micro, top, tok, experts, capacity)
    all_scales4 = all_tables4.astype(jnp.float32) * jnp.swapaxes(gates, 1, 2)[
        :, :, :, None, None
    ]

    def forward_work(tokens, table4, weights, live):
        values, scale, normed = normalize(tokens, gain_row)
        send = jnp.einsum(
            "ktec,td->ecd", table4, normed, preferred_element_type=jnp.float32
        ).astype(jnp.bfloat16)

        def forward_active(operand):
            pre_gate, pre_up = pre_products(operand, weight_gate, weight_up)
            product = (pre_gate * jax.nn.sigmoid(pre_gate) * pre_up).astype(jnp.bfloat16)
            output = jnp.einsum(
                "ech,hd->ecd", product, weight_down, preferred_element_type=jnp.float32
            ).astype(jnp.bfloat16)
            return (output, pre_gate, pre_up)

        def forward_resting(operand):
            pre_zero = jnp.zeros(operand.shape[:-1] + (inner,), jnp.float32)
            return (jnp.zeros_like(operand), pre_zero, pre_zero)

        output, pre_gate, pre_up = lax.cond(
            live,
            forward_active,
            forward_resting,
            lax.all_to_all(send, "expert", split_axis=0, concat_axis=0, tiled=True),
        )
        back = return_rows(output).reshape(total_rows, width)
        mixed = values + jnp.dot(
            weights, back.astype(jnp.float32), precision=lax.Precision.HIGHEST
        )
        return (mixed.astype(jnp.bfloat16), pre_gate, pre_up)

    def forward_tick(carry, tick):
        incoming, outputs, kept_x, kept_gate, kept_up = carry
        offset = tick - section
        live = (offset >= 0) & (offset < micro)
        index = jnp.clip(offset, 0, micro - 1)
        slot = jnp.where(live, offset, micro)
        fresh = lax.dynamic_index_in_dim(inputs, index, 0, keepdims=False)
        tokens = jnp.where(section == 0, fresh, incoming)
        table4 = lax.dynamic_index_in_dim(all_tables4, index, 0, keepdims=False)
        weights = lax.dynamic_index_in_dim(all_weights, index, 0, keepdims=False)
        mixed, pre_gate, pre_up = forward_work(tokens, table4, weights, live)
        outputs = lax.dynamic_update_index_in_dim(outputs, mixed, slot, 0)
        kept_x = lax.dynamic_update_index_in_dim(kept_x, tokens, slot, 0)
        kept_gate = lax.dynamic_update_index_in_dim(
            kept_gate, pre_gate.reshape(total_rows, inner), slot, 0
        )
        kept_up = lax.dynamic_update_index_in_dim(
            kept_up, pre_up.reshape(total_rows, inner), slot, 0
        )
        incoming = passed_along(mixed, "section", 1)
        return ((incoming, outputs, kept_x, kept_gate, kept_up), None)

    spare = (micro + 1,)
    start = (
        jnp.zeros((tok, width), jnp.bfloat16),
        jnp.zeros(spare + inputs.shape[1:], jnp.bfloat16),
        jnp.zeros(spare + inputs.shape[1:], jnp.bfloat16),
        jnp.zeros(spare + (total_rows, inner), jnp.float32),
        jnp.zeros(spare + (total_rows, inner), jnp.float32),
    )
    finished, _ = lax.scan(forward_tick, start, jnp.arange(ticks, dtype=jnp.int32))
    _, outputs, kept_x, kept_gate, kept_up = finished
    down_across = lax.optimization_barrier(jnp.transpose(weight_down))

    def backward_work(tokens, grad_out, table, scales4, gate_kept, up_kept, live):
        values, scale, normed = normalize(tokens, gain_row)
        grad_send = jnp.einsum(
            "ktec,td->ecd",
            scales4,
            grad_out.astype(jnp.float32),
            precision=lax.Precision.HIGHEST,
        ).astype(jnp.bfloat16)

        def backward_active(operands):
            rows_grad, gate_pre, up_pre = operands
            d_hidden = jnp.dot(
                rows_grad.reshape(total_rows, width),
                down_across,
                preferred_element_type=jnp.float32,
            )
            sigma = jax.nn.sigmoid(gate_pre)
            d_gate = (d_hidden * up_pre * sigma * (1.0 + gate_pre * (1.0 - sigma))).astype(
                jnp.bfloat16
            )
            d_up = (d_hidden * gate_pre * sigma).astype(jnp.bfloat16)
            back = contract_last(d_gate, weight_gate) + contract_last(d_up, weight_up)
            return back.astype(jnp.bfloat16).reshape(rows_grad.shape)

        def backward_resting(operands):
            return jnp.zeros_like(operands[0])

        computed = lax.cond(
            live,
            backward_active,
            backward_resting,
            (
                lax.all_to_all(grad_send, "expert", split_axis=0, concat_axis=0, tiled=True),
                gate_kept,
                up_kept,
            ),
        )
        back = return_rows(computed).reshape(total_rows, width)
        d_norm = jnp.einsum("ktj,jd->td", table, back, preferred_element_type=jnp.float32)
        weighted = d_norm * gain_row
        result = (
            grad_out.astype(jnp.float32)
            + scale * weighted
            - values * (scale * scale * scale) * jnp.mean(values * weighted, axis=-1, keepdims=True)
        )
        return result.astype(jnp.bfloat16)

    def backward_tick(carry, tick):
        incoming, results = carry
        offset = tick - (sections - 1 - section)
        live = (offset >= 0) & (offset < micro)
        index = jnp.clip(offset, 0, micro - 1)
        slot = jnp.where(live, offset, micro)
        fresh = lax.dynamic_index_in_dim(cotangent, index, 0, keepdims=False)
        grad_out = jnp.where(section == sections - 1, fresh, incoming)
        tokens = lax.dynamic_index_in_dim(kept_x, index, 0, keepdims=False)
        table = lax.dynamic_index_in_dim(all_tables, index, 0, keepdims=False)
        scales4 = lax.dynamic_index_in_dim(all_scales4, index, 0, keepdims=False)
        gate_kept = lax.dynamic_index_in_dim(kept_gate, index, 0, keepdims=False)
        up_kept = lax.dynamic_index_in_dim(kept_up, index, 0, keepdims=False)
        result = backward_work(
            tokens, grad_out, table, scales4, gate_kept, up_kept, live
        )
        results = lax.dynamic_update_index_in_dim(results, result, slot, 0)
        incoming = passed_along(result, "section", -1)
        return ((incoming, results), None)

    done, _ = lax.scan(
        backward_tick,
        (
            jnp.zeros((tok, width), jnp.bfloat16),
            jnp.zeros(spare + cotangent.shape[1:], jnp.bfloat16),
        ),
        jnp.arange(ticks, dtype=jnp.int32),
    )
    results = done[1]
    return (outputs[None, :micro], results[None, :micro])


def solution(mesh):
    placed = (
        P(None, "expert", None),
        P(None, "expert", None),
        P("section", None),
        P("section", None, "expert", None),
        P("section", None, "expert", None),
        P("section", "expert", None, None),
        P("section", "expert", None, None),
        P("section", "expert", None, None),
    )
    return jax.shard_map(
        local,
        mesh=mesh,
        in_specs=placed,
        out_specs=(P("section", None, "expert", None), P("section", None, "expert", None)),
        check_vma=False,
    )
```

```python
import jax
import jax.numpy as jnp
from jax import lax
from jax.sharding import PartitionSpec as P

EPS = 1e-06


def passed_along(value, axis, steps):
    count = lax.axis_size(axis)
    leading, last = (max(0, -steps), min(count, count - steps))
    return lax.ppermute(value, axis, [(source, source + steps) for source in range(leading, last)])


def slot_places(route, experts, capacity):
    flat = route.reshape(-1)
    onehot = (flat[:, None] == jnp.arange(experts, dtype=jnp.int32)[None, :]).astype(jnp.int32)
    before = jnp.cumsum(onehot, axis=0) - onehot
    slot = jnp.sum(before * onehot, axis=1)
    return (flat * capacity + slot).reshape(route.shape)


def slot_table(places, total_rows):
    grid = jnp.arange(total_rows, dtype=jnp.int32)
    return (places.T[:, :, None] == grid[None, None, :]).astype(jnp.bfloat16)


def normalize(tokens, gain):
    values = tokens.astype(jnp.float32)
    scale = lax.rsqrt(jnp.mean(values * values, axis=-1, keepdims=True) + EPS)
    return (values, scale, (values * scale * gain).astype(jnp.bfloat16))


def pre_products(rows, w_gate, w_up):
    flat = rows.reshape(-1, rows.shape[-1])
    pre_gate = jnp.dot(flat, w_gate, preferred_element_type=jnp.float32)
    pre_up = jnp.dot(flat, w_up, preferred_element_type=jnp.float32)
    inner = rows.shape[:-1] + (w_gate.shape[1],)
    return (pre_gate.reshape(inner), pre_up.reshape(inner))


def expert_forward(rows, w_gate, w_up, w_down):
    pre_gate, pre_up = pre_products(rows, w_gate, w_up)
    width = w_gate.shape[1]
    product = (pre_gate * jax.nn.sigmoid(pre_gate) * pre_up).astype(jnp.bfloat16)
    output = jnp.dot(product.reshape(-1, width), w_down, preferred_element_type=jnp.float32).astype(
        jnp.bfloat16
    )
    return (output.reshape(rows.shape), pre_gate, pre_up)


def contract_last(left, right):
    return lax.dot_general(
        left, right, (((1,), (1,)), ((), ())), preferred_element_type=jnp.float32
    )


def expert_backward(grad_rows, pre_gate, pre_up, w_gate, w_up, w_down):
    shape = grad_rows.shape
    width = w_gate.shape[1]
    flat = grad_rows.reshape(-1, shape[-1])
    gate_pre = pre_gate.reshape(-1, width)
    up_pre = pre_up.reshape(-1, width)
    d_hidden = contract_last(flat, w_down)
    sigma = jax.nn.sigmoid(gate_pre)
    d_gate = (d_hidden * up_pre * sigma * (1.0 + gate_pre * (1.0 - sigma))).astype(jnp.bfloat16)
    d_up = (d_hidden * gate_pre * sigma).astype(jnp.bfloat16)
    back = contract_last(d_gate, w_gate) + contract_last(d_up, w_up)
    return back.astype(jnp.bfloat16).reshape(shape)


def return_rows(rows):
    return lax.all_to_all(rows, "expert", split_axis=0, concat_axis=0, tiled=True)


def local(inputs, cotangent, gain, route, gate, w_gate, w_up, w_down):
    micro, tok, width = inputs.shape
    top = route.shape[-1]
    experts = lax.axis_size("expert")
    capacity = tok * top * 7 // (6 * experts)
    total_rows = experts * capacity
    sections = lax.axis_size("section")
    section = lax.axis_index("section")
    ticks = sections + micro - 1
    gain_row = gain[0]
    weight_gate = w_gate[0, 0]
    weight_up = w_up[0, 0]
    weight_down = w_down[0, 0]
    inner = weight_gate.shape[1]
    routes = route[0]
    gates = gate[0]

    weight_both = jnp.concatenate([weight_gate, weight_up], axis=1)
    all_places = jax.vmap(lambda r: slot_places(r, experts, capacity))(routes)
    all_tables = jax.vmap(lambda p: slot_table(p, total_rows))(all_places)
    all_weights = jnp.einsum(
        "mktj,mtk->mtj", all_tables.astype(jnp.float32), gates, precision=lax.Precision.HIGHEST
    )
    all_tables4 = all_tables.reshape(micro, top, tok, experts, capacity)

    def forward_work(tokens, table4, weights, live):
        values, scale, normed = normalize(tokens, gain_row)
        send = jnp.einsum(
            "ktec,td->ecd", table4, normed, preferred_element_type=jnp.float32
        ).astype(jnp.bfloat16)

        def forward_active(operand):
            pre_both = jnp.dot(
                operand.reshape(total_rows, width), weight_both, preferred_element_type=jnp.float32
            ).reshape(operand.shape[:-1] + (2 * inner,))
            pre_gate = pre_both[..., :inner]
            pre_up = pre_both[..., inner:]
            product = (pre_gate * jax.nn.sigmoid(pre_gate) * pre_up).astype(jnp.bfloat16)
            output = jnp.einsum(
                "ech,hd->ecd", product, weight_down, preferred_element_type=jnp.float32
            ).astype(jnp.bfloat16)
            return (output, pre_gate, pre_up)

        def forward_resting(operand):
            pre_zero = jnp.zeros(operand.shape[:-1] + (inner,), jnp.float32)
            return (jnp.zeros_like(operand), pre_zero, pre_zero)

        output, pre_gate, pre_up = lax.cond(
            live,
            forward_active,
            forward_resting,
            lax.all_to_all(send, "expert", split_axis=0, concat_axis=0, tiled=True),
        )
        back = return_rows(output).reshape(total_rows, width)
        mixed = values + jnp.dot(
            weights, back.astype(jnp.float32), precision=lax.Precision.HIGHEST
        )
        return (mixed.astype(jnp.bfloat16), pre_gate, pre_up)

    def forward_tick(carry, tick):
        incoming, outputs, kept_x, kept_gate, kept_up = carry
        offset = tick - section
        live = (offset >= 0) & (offset < micro)
        index = jnp.clip(offset, 0, micro - 1)
        slot = jnp.where(live, offset, micro)
        fresh = lax.dynamic_index_in_dim(inputs, index, 0, keepdims=False)
        tokens = jnp.where(section == 0, fresh, incoming)
        table4 = lax.dynamic_index_in_dim(all_tables4, index, 0, keepdims=False)
        weights = lax.dynamic_index_in_dim(all_weights, index, 0, keepdims=False)
        mixed, pre_gate, pre_up = forward_work(tokens, table4, weights, live)
        outputs = lax.dynamic_update_index_in_dim(outputs, mixed, slot, 0)
        kept_x = lax.dynamic_update_index_in_dim(kept_x, tokens, slot, 0)
        kept_gate = lax.dynamic_update_index_in_dim(
            kept_gate, pre_gate.reshape(total_rows, inner), slot, 0
        )
        kept_up = lax.dynamic_update_index_in_dim(
            kept_up, pre_up.reshape(total_rows, inner), slot, 0
        )
        incoming = passed_along(mixed, "section", 1)
        return ((incoming, outputs, kept_x, kept_gate, kept_up), None)

    spare = (micro + 1,)
    start = (
        jnp.zeros((tok, width), jnp.bfloat16),
        jnp.zeros(spare + inputs.shape[1:], jnp.bfloat16),
        jnp.zeros(spare + inputs.shape[1:], jnp.bfloat16),
        jnp.zeros(spare + (total_rows, inner), jnp.float32),
        jnp.zeros(spare + (total_rows, inner), jnp.float32),
    )
    finished, _ = lax.scan(forward_tick, start, jnp.arange(ticks, dtype=jnp.int32))
    _, outputs, kept_x, kept_gate, kept_up = finished
    down_across = lax.optimization_barrier(jnp.transpose(weight_down))

    def backward_work(tokens, grad_out, table, table4, gate_now, gate_kept, up_kept, live):
        values, scale, normed = normalize(tokens, gain_row)
        scaled = (gate_now[..., None] * grad_out.astype(jnp.float32)[:, None, :]).astype(
            jnp.bfloat16
        )
        grad_send = jnp.einsum(
            "ktec,tkd->ecd", table4, scaled, preferred_element_type=jnp.float32
        ).astype(jnp.bfloat16)

        def backward_active(operands):
            rows_grad, gate_pre, up_pre = operands
            d_hidden = jnp.dot(
                rows_grad.reshape(total_rows, width),
                down_across,
                preferred_element_type=jnp.float32,
            )
            sigma = jax.nn.sigmoid(gate_pre)
            d_gate = (d_hidden * up_pre * sigma * (1.0 + gate_pre * (1.0 - sigma))).astype(
                jnp.bfloat16
            )
            d_up = (d_hidden * gate_pre * sigma).astype(jnp.bfloat16)
            back = contract_last(jnp.concatenate([d_gate, d_up], axis=-1), weight_both)
            return back.astype(jnp.bfloat16).reshape(rows_grad.shape)

        def backward_resting(operands):
            return jnp.zeros_like(operands[0])

        computed = lax.cond(
            live,
            backward_active,
            backward_resting,
            (
                lax.all_to_all(grad_send, "expert", split_axis=0, concat_axis=0, tiled=True),
                gate_kept,
                up_kept,
            ),
        )
        back = return_rows(computed).reshape(total_rows, width)
        d_norm = jnp.einsum("ktj,jd->td", table, back, preferred_element_type=jnp.float32)
        weighted = d_norm * gain_row
        result = (
            grad_out.astype(jnp.float32)
            + scale * weighted
            - values * (scale * scale * scale) * jnp.mean(values * weighted, axis=-1, keepdims=True)
        )
        return result.astype(jnp.bfloat16)

    def backward_tick(carry, tick):
        incoming, results = carry
        offset = tick - (sections - 1 - section)
        live = (offset >= 0) & (offset < micro)
        index = jnp.clip(offset, 0, micro - 1)
        slot = jnp.where(live, offset, micro)
        fresh = lax.dynamic_index_in_dim(cotangent, index, 0, keepdims=False)
        grad_out = jnp.where(section == sections - 1, fresh, incoming)
        tokens = lax.dynamic_index_in_dim(kept_x, index, 0, keepdims=False)
        table = lax.dynamic_index_in_dim(all_tables, index, 0, keepdims=False)
        table4 = lax.dynamic_index_in_dim(all_tables4, index, 0, keepdims=False)
        gate_now = lax.dynamic_index_in_dim(gates, index, 0, keepdims=False)
        gate_kept = lax.dynamic_index_in_dim(kept_gate, index, 0, keepdims=False)
        up_kept = lax.dynamic_index_in_dim(kept_up, index, 0, keepdims=False)
        result = backward_work(
            tokens, grad_out, table, table4, gate_now, gate_kept, up_kept, live
        )
        results = lax.dynamic_update_index_in_dim(results, result, slot, 0)
        incoming = passed_along(result, "section", -1)
        return ((incoming, results), None)

    done, _ = lax.scan(
        backward_tick,
        (
            jnp.zeros((tok, width), jnp.bfloat16),
            jnp.zeros(spare + cotangent.shape[1:], jnp.bfloat16),
        ),
        jnp.arange(ticks, dtype=jnp.int32),
    )
    results = done[1]
    return (outputs[None, :micro], results[None, :micro])


def solution(mesh):
    placed = (
        P(None, "expert", None),
        P(None, "expert", None),
        P("section", None),
        P("section", None, "expert", None),
        P("section", None, "expert", None),
        P("section", "expert", None, None),
        P("section", "expert", None, None),
        P("section", "expert", None, None),
    )
    return jax.shard_map(
        local,
        mesh=mesh,
        in_specs=placed,
        out_specs=(P("section", None, "expert", None), P("section", None, "expert", None)),
        check_vma=False,
    )
```

```python
import jax
import jax.numpy as jnp
from jax import lax
from jax.sharding import PartitionSpec as P

EPS = 1e-06


def passed_along(value, axis, steps):
    count = lax.axis_size(axis)
    leading, last = (max(0, -steps), min(count, count - steps))
    return lax.ppermute(value, axis, [(source, source + steps) for source in range(leading, last)])


def slot_places(route, experts, capacity):
    flat = route.reshape(-1)
    onehot = (flat[:, None] == jnp.arange(experts, dtype=jnp.int32)[None, :]).astype(jnp.int32)
    before = jnp.cumsum(onehot, axis=0) - onehot
    slot = jnp.sum(before * onehot, axis=1)
    return (flat * capacity + slot).reshape(route.shape)


def slot_table(places, total_rows):
    grid = jnp.arange(total_rows, dtype=jnp.int32)
    return (places.T[:, :, None] == grid[None, None, :]).astype(jnp.bfloat16)


def normalize(tokens, gain):
    values = tokens.astype(jnp.float32)
    scale = lax.rsqrt(jnp.mean(values * values, axis=-1, keepdims=True) + EPS)
    return (values, scale, (values * scale * gain).astype(jnp.bfloat16))


def pre_products(rows, w_gate, w_up):
    flat = rows.reshape(-1, rows.shape[-1])
    pre_gate = jnp.dot(flat, w_gate, preferred_element_type=jnp.float32)
    pre_up = jnp.dot(flat, w_up, preferred_element_type=jnp.float32)
    inner = rows.shape[:-1] + (w_gate.shape[1],)
    return (pre_gate.reshape(inner), pre_up.reshape(inner))


def expert_forward(rows, w_gate, w_up, w_down):
    pre_gate, pre_up = pre_products(rows, w_gate, w_up)
    width = w_gate.shape[1]
    product = (pre_gate * jax.nn.sigmoid(pre_gate) * pre_up).astype(jnp.bfloat16)
    output = jnp.dot(product.reshape(-1, width), w_down, preferred_element_type=jnp.float32).astype(
        jnp.bfloat16
    )
    return (output.reshape(rows.shape), pre_gate, pre_up)


def contract_last(left, right):
    return lax.dot_general(
        left, right, (((1,), (1,)), ((), ())), preferred_element_type=jnp.float32
    )


def expert_backward(grad_rows, pre_gate, pre_up, w_gate, w_up, w_down):
    shape = grad_rows.shape
    width = w_gate.shape[1]
    flat = grad_rows.reshape(-1, shape[-1])
    gate_pre = pre_gate.reshape(-1, width)
    up_pre = pre_up.reshape(-1, width)
    d_hidden = contract_last(flat, w_down)
    sigma = jax.nn.sigmoid(gate_pre)
    d_gate = (d_hidden * up_pre * sigma * (1.0 + gate_pre * (1.0 - sigma))).astype(jnp.bfloat16)
    d_up = (d_hidden * gate_pre * sigma).astype(jnp.bfloat16)
    back = contract_last(d_gate, w_gate) + contract_last(d_up, w_up)
    return back.astype(jnp.bfloat16).reshape(shape)


def return_rows(rows):
    return lax.all_to_all(rows, "expert", split_axis=0, concat_axis=0, tiled=True)


def local(inputs, cotangent, gain, route, gate, w_gate, w_up, w_down):
    micro, tok, width = inputs.shape
    top = route.shape[-1]
    experts = lax.axis_size("expert")
    capacity = tok * top * 7 // (6 * experts)
    total_rows = experts * capacity
    sections = lax.axis_size("section")
    section = lax.axis_index("section")
    ticks = sections + micro - 1
    gain_row = gain[0]
    weight_gate = w_gate[0, 0]
    weight_up = w_up[0, 0]
    weight_down = w_down[0, 0]
    inner = weight_gate.shape[1]
    routes = route[0]
    gates = gate[0]

    all_places = jax.vmap(lambda r: slot_places(r, experts, capacity))(routes)
    all_tables = jax.vmap(lambda p: slot_table(p, total_rows))(all_places)
    all_weights = jnp.einsum(
        "mktj,mtk->mtj", all_tables.astype(jnp.float32), gates, precision=lax.Precision.HIGHEST
    )
    all_tables4 = all_tables.reshape(micro, top, tok, experts, capacity)
    pair_ids = jnp.arange(top * tok, dtype=jnp.float32).reshape(top, tok)
    token_ids = jnp.broadcast_to(jnp.arange(tok, dtype=jnp.float32)[None, :], (top, tok))
    filled = jnp.sum(all_tables4.astype(jnp.float32), axis=(1, 2))
    empty = jnp.float32(top * tok)
    all_token_src = jnp.where(
        filled > 0,
        jnp.einsum("mktec,kt->mec", all_tables4.astype(jnp.float32), token_ids),
        empty,
    ).astype(jnp.int32)
    all_pair_src = jnp.where(
        filled > 0,
        jnp.einsum("mktec,kt->mec", all_tables4.astype(jnp.float32), pair_ids),
        empty,
    ).astype(jnp.int32)

    def forward_work(tokens, token_src, weights, live):
        values, scale, normed = normalize(tokens, gain_row)
        send = jnp.take(normed, token_src, axis=0, mode="fill", fill_value=0)

        def forward_active(operand):
            pre_gate, pre_up = pre_products(operand, weight_gate, weight_up)
            product = (pre_gate * jax.nn.sigmoid(pre_gate) * pre_up).astype(jnp.bfloat16)
            output = jnp.einsum(
                "ech,hd->ecd", product, weight_down, preferred_element_type=jnp.float32
            ).astype(jnp.bfloat16)
            return (output, pre_gate, pre_up)

        def forward_resting(operand):
            pre_zero = jnp.zeros(operand.shape[:-1] + (inner,), jnp.float32)
            return (jnp.zeros_like(operand), pre_zero, pre_zero)

        output, pre_gate, pre_up = lax.cond(
            live,
            forward_active,
            forward_resting,
            lax.all_to_all(send, "expert", split_axis=0, concat_axis=0, tiled=True),
        )
        back = return_rows(output).reshape(total_rows, width)
        mixed = values + jnp.dot(
            weights, back.astype(jnp.float32), precision=lax.Precision.HIGHEST
        )
        return (mixed.astype(jnp.bfloat16), pre_gate, pre_up)

    def forward_tick(carry, tick):
        incoming, outputs, kept_x, kept_gate, kept_up = carry
        offset = tick - section
        live = (offset >= 0) & (offset < micro)
        index = jnp.clip(offset, 0, micro - 1)
        slot = jnp.where(live, offset, micro)
        fresh = lax.dynamic_index_in_dim(inputs, index, 0, keepdims=False)
        tokens = jnp.where(section == 0, fresh, incoming)
        token_src = lax.dynamic_index_in_dim(all_token_src, index, 0, keepdims=False)
        weights = lax.dynamic_index_in_dim(all_weights, index, 0, keepdims=False)
        mixed, pre_gate, pre_up = forward_work(tokens, token_src, weights, live)
        outputs = lax.dynamic_update_index_in_dim(outputs, mixed, slot, 0)
        kept_x = lax.dynamic_update_index_in_dim(kept_x, tokens, slot, 0)
        kept_gate = lax.dynamic_update_index_in_dim(
            kept_gate, pre_gate.reshape(total_rows, inner), slot, 0
        )
        kept_up = lax.dynamic_update_index_in_dim(
            kept_up, pre_up.reshape(total_rows, inner), slot, 0
        )
        incoming = passed_along(mixed, "section", 1)
        return ((incoming, outputs, kept_x, kept_gate, kept_up), None)

    spare = (micro + 1,)
    start = (
        jnp.zeros((tok, width), jnp.bfloat16),
        jnp.zeros(spare + inputs.shape[1:], jnp.bfloat16),
        jnp.zeros(spare + inputs.shape[1:], jnp.bfloat16),
        jnp.zeros(spare + (total_rows, inner), jnp.float32),
        jnp.zeros(spare + (total_rows, inner), jnp.float32),
    )
    finished, _ = lax.scan(forward_tick, start, jnp.arange(ticks, dtype=jnp.int32))
    _, outputs, kept_x, kept_gate, kept_up = finished
    down_across = lax.optimization_barrier(jnp.transpose(weight_down))

    def backward_work(tokens, grad_out, table, pair_src, gate_now, gate_kept, up_kept, live):
        values, scale, normed = normalize(tokens, gain_row)
        scaled = (gate_now[..., None] * grad_out.astype(jnp.float32)[:, None, :]).astype(
            jnp.bfloat16
        )
        pairs = jnp.swapaxes(scaled, 0, 1).reshape(top * tok, width)
        grad_send = jnp.take(pairs, pair_src, axis=0, mode="fill", fill_value=0)

        def backward_active(operands):
            rows_grad, gate_pre, up_pre = operands
            d_hidden = jnp.dot(
                rows_grad.reshape(total_rows, width),
                down_across,
                preferred_element_type=jnp.float32,
            )
            sigma = jax.nn.sigmoid(gate_pre)
            d_gate = (d_hidden * up_pre * sigma * (1.0 + gate_pre * (1.0 - sigma))).astype(
                jnp.bfloat16
            )
            d_up = (d_hidden * gate_pre * sigma).astype(jnp.bfloat16)
            back = contract_last(d_gate, weight_gate) + contract_last(d_up, weight_up)
            return back.astype(jnp.bfloat16).reshape(rows_grad.shape)

        def backward_resting(operands):
            return jnp.zeros_like(operands[0])

        computed = lax.cond(
            live,
            backward_active,
            backward_resting,
            (
                lax.all_to_all(grad_send, "expert", split_axis=0, concat_axis=0, tiled=True),
                gate_kept,
                up_kept,
            ),
        )
        back = return_rows(computed).reshape(total_rows, width)
        d_norm = jnp.einsum("ktj,jd->td", table, back, preferred_element_type=jnp.float32)
        weighted = d_norm * gain_row
        result = (
            grad_out.astype(jnp.float32)
            + scale * weighted
            - values * (scale * scale * scale) * jnp.mean(values * weighted, axis=-1, keepdims=True)
        )
        return result.astype(jnp.bfloat16)

    def backward_tick(carry, tick):
        incoming, results = carry
        offset = tick - (sections - 1 - section)
        live = (offset >= 0) & (offset < micro)
        index = jnp.clip(offset, 0, micro - 1)
        slot = jnp.where(live, offset, micro)
        fresh = lax.dynamic_index_in_dim(cotangent, index, 0, keepdims=False)
        grad_out = jnp.where(section == sections - 1, fresh, incoming)
        tokens = lax.dynamic_index_in_dim(kept_x, index, 0, keepdims=False)
        table = lax.dynamic_index_in_dim(all_tables, index, 0, keepdims=False)
        pair_src = lax.dynamic_index_in_dim(all_pair_src, index, 0, keepdims=False)
        gate_now = lax.dynamic_index_in_dim(gates, index, 0, keepdims=False)
        gate_kept = lax.dynamic_index_in_dim(kept_gate, index, 0, keepdims=False)
        up_kept = lax.dynamic_index_in_dim(kept_up, index, 0, keepdims=False)
        result = backward_work(
            tokens, grad_out, table, pair_src, gate_now, gate_kept, up_kept, live
        )
        results = lax.dynamic_update_index_in_dim(results, result, slot, 0)
        incoming = passed_along(result, "section", -1)
        return ((incoming, results), None)

    done, _ = lax.scan(
        backward_tick,
        (
            jnp.zeros((tok, width), jnp.bfloat16),
            jnp.zeros(spare + cotangent.shape[1:], jnp.bfloat16),
        ),
        jnp.arange(ticks, dtype=jnp.int32),
    )
    results = done[1]
    return (outputs[None, :micro], results[None, :micro])


def solution(mesh):
    placed = (
        P(None, "expert", None),
        P(None, "expert", None),
        P("section", None),
        P("section", None, "expert", None),
        P("section", None, "expert", None),
        P("section", "expert", None, None),
        P("section", "expert", None, None),
        P("section", "expert", None, None),
    )
    return jax.shard_map(
        local,
        mesh=mesh,
        in_specs=placed,
        out_specs=(P("section", None, "expert", None), P("section", None, "expert", None)),
        check_vma=False,
    )
```

```python
import jax
import jax.numpy as jnp
from jax import lax
from jax.sharding import PartitionSpec as P

EPS = 1e-06


def passed_along(value, axis, steps):
    count = lax.axis_size(axis)
    leading, last = (max(0, -steps), min(count, count - steps))
    return lax.ppermute(value, axis, [(source, source + steps) for source in range(leading, last)])


def slot_places(route, experts, capacity):
    flat = route.reshape(-1)
    onehot = (flat[:, None] == jnp.arange(experts, dtype=jnp.int32)[None, :]).astype(jnp.int32)
    before = jnp.cumsum(onehot, axis=0) - onehot
    slot = jnp.sum(before * onehot, axis=1)
    return (flat * capacity + slot).reshape(route.shape)


def slot_table(places, total_rows):
    grid = jnp.arange(total_rows, dtype=jnp.int32)
    return (places.T[:, :, None] == grid[None, None, :]).astype(jnp.bfloat16)


def normalize(tokens, gain):
    values = tokens.astype(jnp.float32)
    scale = lax.rsqrt(jnp.mean(values * values, axis=-1, keepdims=True) + EPS)
    return (values, scale, (values * scale * gain).astype(jnp.bfloat16))


def pre_products(rows, w_gate, w_up):
    flat = rows.reshape(-1, rows.shape[-1])
    pre_gate = jnp.dot(flat, w_gate, preferred_element_type=jnp.float32)
    pre_up = jnp.dot(flat, w_up, preferred_element_type=jnp.float32)
    inner = rows.shape[:-1] + (w_gate.shape[1],)
    return (pre_gate.reshape(inner), pre_up.reshape(inner))


def expert_forward(rows, w_gate, w_up, w_down):
    pre_gate, pre_up = pre_products(rows, w_gate, w_up)
    width = w_gate.shape[1]
    product = (pre_gate * jax.nn.sigmoid(pre_gate) * pre_up).astype(jnp.bfloat16)
    output = jnp.dot(product.reshape(-1, width), w_down, preferred_element_type=jnp.float32).astype(
        jnp.bfloat16
    )
    return (output.reshape(rows.shape), pre_gate, pre_up)


def contract_last(left, right):
    return lax.dot_general(
        left, right, (((1,), (1,)), ((), ())), preferred_element_type=jnp.float32
    )


def expert_backward(grad_rows, pre_gate, pre_up, w_gate, w_up, w_down):
    shape = grad_rows.shape
    width = w_gate.shape[1]
    flat = grad_rows.reshape(-1, shape[-1])
    gate_pre = pre_gate.reshape(-1, width)
    up_pre = pre_up.reshape(-1, width)
    d_hidden = contract_last(flat, w_down)
    sigma = jax.nn.sigmoid(gate_pre)
    d_gate = (d_hidden * up_pre * sigma * (1.0 + gate_pre * (1.0 - sigma))).astype(jnp.bfloat16)
    d_up = (d_hidden * gate_pre * sigma).astype(jnp.bfloat16)
    back = contract_last(d_gate, w_gate) + contract_last(d_up, w_up)
    return back.astype(jnp.bfloat16).reshape(shape)


def return_rows(rows):
    return lax.all_to_all(rows, "expert", split_axis=0, concat_axis=0, tiled=True)


def local(inputs, cotangent, gain, route, gate, w_gate, w_up, w_down):
    micro, tok, width = inputs.shape
    top = route.shape[-1]
    experts = lax.axis_size("expert")
    capacity = tok * top * 7 // (6 * experts)
    total_rows = experts * capacity
    sections = lax.axis_size("section")
    section = lax.axis_index("section")
    ticks = sections + micro - 1
    gain_row = gain[0]
    weight_gate = w_gate[0, 0]
    weight_up = w_up[0, 0]
    weight_down = w_down[0, 0]
    inner = weight_gate.shape[1]
    routes = route[0]
    gates = gate[0]

    all_places = jax.vmap(lambda r: slot_places(r, experts, capacity))(routes)
    all_tables = jax.vmap(lambda p: slot_table(p, total_rows))(all_places)
    all_weights = jnp.einsum(
        "mktj,mtk->mtj", all_tables.astype(jnp.float32), gates, precision=lax.Precision.HIGHEST
    )
    all_tables4 = all_tables.reshape(micro, top, tok, experts, capacity)

    def forward_work(tokens, table4, table, gate_now, live):
        values, scale, normed = normalize(tokens, gain_row)
        send = jnp.einsum(
            "ktec,td->ecd", table4, normed, preferred_element_type=jnp.float32
        ).astype(jnp.bfloat16)

        def forward_active(operand):
            pre_gate, pre_up = pre_products(operand, weight_gate, weight_up)
            product = (pre_gate * jax.nn.sigmoid(pre_gate) * pre_up).astype(jnp.bfloat16)
            output = jnp.einsum(
                "ech,hd->ecd", product, weight_down, preferred_element_type=jnp.float32
            ).astype(jnp.bfloat16)
            return (output, pre_gate, pre_up)

        def forward_resting(operand):
            pre_zero = jnp.zeros(operand.shape[:-1] + (inner,), jnp.float32)
            return (jnp.zeros_like(operand), pre_zero, pre_zero)

        output, pre_gate, pre_up = lax.cond(
            live,
            forward_active,
            forward_resting,
            lax.all_to_all(send, "expert", split_axis=0, concat_axis=0, tiled=True),
        )
        back = return_rows(output).reshape(total_rows, width)
        picked = jnp.einsum("ktj,jd->tkd", table, back, preferred_element_type=jnp.float32)
        mixed = values + jnp.sum(gate_now[..., None] * picked, axis=1)
        return (mixed.astype(jnp.bfloat16), pre_gate, pre_up)

    def forward_tick(carry, tick):
        incoming, outputs, kept_x, kept_gate, kept_up = carry
        offset = tick - section
        live = (offset >= 0) & (offset < micro)
        index = jnp.clip(offset, 0, micro - 1)
        slot = jnp.where(live, offset, micro)
        fresh = lax.dynamic_index_in_dim(inputs, index, 0, keepdims=False)
        tokens = jnp.where(section == 0, fresh, incoming)
        table4 = lax.dynamic_index_in_dim(all_tables4, index, 0, keepdims=False)
        table = lax.dynamic_index_in_dim(all_tables, index, 0, keepdims=False)
        gate_now = lax.dynamic_index_in_dim(gates, index, 0, keepdims=False)
        mixed, pre_gate, pre_up = forward_work(tokens, table4, table, gate_now, live)
        outputs = lax.dynamic_update_index_in_dim(outputs, mixed, slot, 0)
        kept_x = lax.dynamic_update_index_in_dim(kept_x, tokens, slot, 0)
        kept_gate = lax.dynamic_update_index_in_dim(
            kept_gate, pre_gate.reshape(total_rows, inner), slot, 0
        )
        kept_up = lax.dynamic_update_index_in_dim(
            kept_up, pre_up.reshape(total_rows, inner), slot, 0
        )
        incoming = passed_along(mixed, "section", 1)
        return ((incoming, outputs, kept_x, kept_gate, kept_up), None)

    spare = (micro + 1,)
    start = (
        jnp.zeros((tok, width), jnp.bfloat16),
        jnp.zeros(spare + inputs.shape[1:], jnp.bfloat16),
        jnp.zeros(spare + inputs.shape[1:], jnp.bfloat16),
        jnp.zeros(spare + (total_rows, inner), jnp.float32),
        jnp.zeros(spare + (total_rows, inner), jnp.float32),
    )
    finished, _ = lax.scan(forward_tick, start, jnp.arange(ticks, dtype=jnp.int32))
    _, outputs, kept_x, kept_gate, kept_up = finished
    down_across = lax.optimization_barrier(jnp.transpose(weight_down))

    def backward_work(tokens, grad_out, table, table4, gate_now, gate_kept, up_kept, live):
        values, scale, normed = normalize(tokens, gain_row)
        scaled = (gate_now[..., None] * grad_out.astype(jnp.float32)[:, None, :]).astype(
            jnp.bfloat16
        )
        grad_send = jnp.einsum(
            "ktec,tkd->ecd", table4, scaled, preferred_element_type=jnp.float32
        ).astype(jnp.bfloat16)

        def backward_active(operands):
            rows_grad, gate_pre, up_pre = operands
            d_hidden = jnp.dot(
                rows_grad.reshape(total_rows, width),
                down_across,
                preferred_element_type=jnp.float32,
            )
            sigma = jax.nn.sigmoid(gate_pre)
            d_gate = (d_hidden * up_pre * sigma * (1.0 + gate_pre * (1.0 - sigma))).astype(
                jnp.bfloat16
            )
            d_up = (d_hidden * gate_pre * sigma).astype(jnp.bfloat16)
            back = contract_last(d_gate, weight_gate) + contract_last(d_up, weight_up)
            return back.astype(jnp.bfloat16).reshape(rows_grad.shape)

        def backward_resting(operands):
            return jnp.zeros_like(operands[0])

        computed = lax.cond(
            live,
            backward_active,
            backward_resting,
            (
                lax.all_to_all(grad_send, "expert", split_axis=0, concat_axis=0, tiled=True),
                gate_kept,
                up_kept,
            ),
        )
        back = return_rows(computed).reshape(total_rows, width)
        d_norm = jnp.einsum("ktj,jd->td", table, back, preferred_element_type=jnp.float32)
        weighted = d_norm * gain_row
        result = (
            grad_out.astype(jnp.float32)
            + scale * weighted
            - values * (scale * scale * scale) * jnp.mean(values * weighted, axis=-1, keepdims=True)
        )
        return result.astype(jnp.bfloat16)

    def backward_tick(carry, tick):
        incoming, results = carry
        offset = tick - (sections - 1 - section)
        live = (offset >= 0) & (offset < micro)
        index = jnp.clip(offset, 0, micro - 1)
        slot = jnp.where(live, offset, micro)
        fresh = lax.dynamic_index_in_dim(cotangent, index, 0, keepdims=False)
        grad_out = jnp.where(section == sections - 1, fresh, incoming)
        tokens = lax.dynamic_index_in_dim(kept_x, index, 0, keepdims=False)
        table = lax.dynamic_index_in_dim(all_tables, index, 0, keepdims=False)
        table4 = lax.dynamic_index_in_dim(all_tables4, index, 0, keepdims=False)
        gate_now = lax.dynamic_index_in_dim(gates, index, 0, keepdims=False)
        gate_kept = lax.dynamic_index_in_dim(kept_gate, index, 0, keepdims=False)
        up_kept = lax.dynamic_index_in_dim(kept_up, index, 0, keepdims=False)
        result = backward_work(
            tokens, grad_out, table, table4, gate_now, gate_kept, up_kept, live
        )
        results = lax.dynamic_update_index_in_dim(results, result, slot, 0)
        incoming = passed_along(result, "section", -1)
        return ((incoming, results), None)

    done, _ = lax.scan(
        backward_tick,
        (
            jnp.zeros((tok, width), jnp.bfloat16),
            jnp.zeros(spare + cotangent.shape[1:], jnp.bfloat16),
        ),
        jnp.arange(ticks, dtype=jnp.int32),
    )
    results = done[1]
    return (outputs[None, :micro], results[None, :micro])


def solution(mesh):
    placed = (
        P(None, "expert", None),
        P(None, "expert", None),
        P("section", None),
        P("section", None, "expert", None),
        P("section", None, "expert", None),
        P("section", "expert", None, None),
        P("section", "expert", None, None),
        P("section", "expert", None, None),
    )
    return jax.shard_map(
        local,
        mesh=mesh,
        in_specs=placed,
        out_specs=(P("section", None, "expert", None), P("section", None, "expert", None)),
        check_vma=False,
    )
```

```python
import jax
import jax.numpy as jnp
from jax import lax
from jax.sharding import PartitionSpec as P

EPS = 1e-06


def passed_along(value, axis, steps):
    count = lax.axis_size(axis)
    leading, last = (max(0, -steps), min(count, count - steps))
    return lax.ppermute(value, axis, [(source, source + steps) for source in range(leading, last)])


def slot_places(route, experts, capacity):
    flat = route.reshape(-1)
    onehot = (flat[:, None] == jnp.arange(experts, dtype=jnp.int32)[None, :]).astype(jnp.int32)
    before = jnp.cumsum(onehot, axis=0) - onehot
    slot = jnp.sum(before * onehot, axis=1)
    return (flat * capacity + slot).reshape(route.shape)


def slot_table(places, total_rows):
    grid = jnp.arange(total_rows, dtype=jnp.int32)
    return (places.T[:, :, None] == grid[None, None, :]).astype(jnp.bfloat16)


def normalize(tokens, gain):
    values = tokens.astype(jnp.float32)
    scale = lax.rsqrt(jnp.mean(values * values, axis=-1, keepdims=True) + EPS)
    return (values, scale, (values * scale * gain).astype(jnp.bfloat16))


def pre_products(rows, w_gate, w_up):
    flat = rows.reshape(-1, rows.shape[-1])
    pre_gate = jnp.dot(flat, w_gate, preferred_element_type=jnp.float32)
    pre_up = jnp.dot(flat, w_up, preferred_element_type=jnp.float32)
    inner = rows.shape[:-1] + (w_gate.shape[1],)
    return (pre_gate.reshape(inner), pre_up.reshape(inner))


def expert_forward(rows, w_gate, w_up, w_down):
    pre_gate, pre_up = pre_products(rows, w_gate, w_up)
    width = w_gate.shape[1]
    product = (pre_gate * jax.nn.sigmoid(pre_gate) * pre_up).astype(jnp.bfloat16)
    output = jnp.dot(product.reshape(-1, width), w_down, preferred_element_type=jnp.float32).astype(
        jnp.bfloat16
    )
    return (output.reshape(rows.shape), pre_gate, pre_up)


def contract_last(left, right):
    return lax.dot_general(
        left, right, (((1,), (1,)), ((), ())), preferred_element_type=jnp.float32
    )


def expert_backward(grad_rows, pre_gate, pre_up, w_gate, w_up, w_down):
    shape = grad_rows.shape
    width = w_gate.shape[1]
    flat = grad_rows.reshape(-1, shape[-1])
    gate_pre = pre_gate.reshape(-1, width)
    up_pre = pre_up.reshape(-1, width)
    d_hidden = contract_last(flat, w_down)
    sigma = jax.nn.sigmoid(gate_pre)
    d_gate = (d_hidden * up_pre * sigma * (1.0 + gate_pre * (1.0 - sigma))).astype(jnp.bfloat16)
    d_up = (d_hidden * gate_pre * sigma).astype(jnp.bfloat16)
    back = contract_last(d_gate, w_gate) + contract_last(d_up, w_up)
    return back.astype(jnp.bfloat16).reshape(shape)


def return_rows(rows):
    return lax.all_to_all(rows, "expert", split_axis=0, concat_axis=0, tiled=True)


def local(inputs, cotangent, gain, route, gate, w_gate, w_up, w_down):
    micro, tok, width = inputs.shape
    top = route.shape[-1]
    experts = lax.axis_size("expert")
    capacity = tok * top * 7 // (6 * experts)
    total_rows = experts * capacity
    sections = lax.axis_size("section")
    section = lax.axis_index("section")
    ticks = sections + micro - 1
    gain_row = gain[0]
    weight_gate = w_gate[0, 0]
    weight_up = w_up[0, 0]
    weight_down = w_down[0, 0]
    inner = weight_gate.shape[1]
    routes = route[0]
    gates = gate[0]

    all_places = jax.vmap(lambda r: slot_places(r, experts, capacity))(routes)
    all_tables = jax.vmap(lambda p: slot_table(p, total_rows))(all_places)
    all_weights = jnp.einsum(
        "mktj,mtk->mtj", all_tables.astype(jnp.float32), gates, precision=lax.Precision.HIGHEST
    )
    all_tables4 = all_tables.reshape(micro, top, tok, experts, capacity)
    all_scales4 = all_tables4.astype(jnp.float32) * jnp.swapaxes(gates, 1, 2)[
        :, :, :, None, None
    ]

    def forward_work(tokens, table4, table, gate_now, live):
        values, scale, normed = normalize(tokens, gain_row)
        send = jnp.einsum(
            "ktec,td->ecd", table4, normed, preferred_element_type=jnp.float32
        ).astype(jnp.bfloat16)

        def forward_active(operand):
            pre_gate, pre_up = pre_products(operand, weight_gate, weight_up)
            product = (pre_gate * jax.nn.sigmoid(pre_gate) * pre_up).astype(jnp.bfloat16)
            output = jnp.einsum(
                "ech,hd->ecd", product, weight_down, preferred_element_type=jnp.float32
            ).astype(jnp.bfloat16)
            return (output, pre_gate, pre_up)

        def forward_resting(operand):
            pre_zero = jnp.zeros(operand.shape[:-1] + (inner,), jnp.float32)
            return (jnp.zeros_like(operand), pre_zero, pre_zero)

        output, pre_gate, pre_up = lax.cond(
            live,
            forward_active,
            forward_resting,
            lax.all_to_all(send, "expert", split_axis=0, concat_axis=0, tiled=True),
        )
        back = return_rows(output).reshape(total_rows, width)
        picked = jnp.einsum("ktj,jd->tkd", table, back, preferred_element_type=jnp.float32)
        mixed = values + jnp.sum(gate_now[..., None] * picked, axis=1)
        return (mixed.astype(jnp.bfloat16), pre_gate, pre_up)

    def forward_tick(carry, tick):
        incoming, outputs, kept_x, kept_gate, kept_up = carry
        offset = tick - section
        live = (offset >= 0) & (offset < micro)
        index = jnp.clip(offset, 0, micro - 1)
        slot = jnp.where(live, offset, micro)
        fresh = lax.dynamic_index_in_dim(inputs, index, 0, keepdims=False)
        tokens = jnp.where(section == 0, fresh, incoming)
        table4 = lax.dynamic_index_in_dim(all_tables4, index, 0, keepdims=False)
        table = lax.dynamic_index_in_dim(all_tables, index, 0, keepdims=False)
        gate_now = lax.dynamic_index_in_dim(gates, index, 0, keepdims=False)
        mixed, pre_gate, pre_up = forward_work(tokens, table4, table, gate_now, live)
        outputs = lax.dynamic_update_index_in_dim(outputs, mixed, slot, 0)
        kept_x = lax.dynamic_update_index_in_dim(kept_x, tokens, slot, 0)
        kept_gate = lax.dynamic_update_index_in_dim(
            kept_gate, pre_gate.reshape(total_rows, inner), slot, 0
        )
        kept_up = lax.dynamic_update_index_in_dim(
            kept_up, pre_up.reshape(total_rows, inner), slot, 0
        )
        incoming = passed_along(mixed, "section", 1)
        return ((incoming, outputs, kept_x, kept_gate, kept_up), None)

    spare = (micro + 1,)
    start = (
        jnp.zeros((tok, width), jnp.bfloat16),
        jnp.zeros(spare + inputs.shape[1:], jnp.bfloat16),
        jnp.zeros(spare + inputs.shape[1:], jnp.bfloat16),
        jnp.zeros(spare + (total_rows, inner), jnp.float32),
        jnp.zeros(spare + (total_rows, inner), jnp.float32),
    )
    finished, _ = lax.scan(forward_tick, start, jnp.arange(ticks, dtype=jnp.int32))
    _, outputs, kept_x, kept_gate, kept_up = finished
    down_across = lax.optimization_barrier(jnp.transpose(weight_down))

    def backward_work(tokens, grad_out, table, scales4, gate_kept, up_kept, live):
        values, scale, normed = normalize(tokens, gain_row)
        grad_send = jnp.einsum(
            "ktec,td->ecd",
            scales4,
            grad_out.astype(jnp.float32),
            precision=lax.Precision.HIGHEST,
        ).astype(jnp.bfloat16)

        def backward_active(operands):
            rows_grad, gate_pre, up_pre = operands
            d_hidden = jnp.dot(
                rows_grad.reshape(total_rows, width),
                down_across,
                preferred_element_type=jnp.float32,
            )
            sigma = jax.nn.sigmoid(gate_pre)
            d_gate = (d_hidden * up_pre * sigma * (1.0 + gate_pre * (1.0 - sigma))).astype(
                jnp.bfloat16
            )
            d_up = (d_hidden * gate_pre * sigma).astype(jnp.bfloat16)
            back = contract_last(d_gate, weight_gate) + contract_last(d_up, weight_up)
            return back.astype(jnp.bfloat16).reshape(rows_grad.shape)

        def backward_resting(operands):
            return jnp.zeros_like(operands[0])

        computed = lax.cond(
            live,
            backward_active,
            backward_resting,
            (
                lax.all_to_all(grad_send, "expert", split_axis=0, concat_axis=0, tiled=True),
                gate_kept,
                up_kept,
            ),
        )
        back = return_rows(computed).reshape(total_rows, width)
        d_norm = jnp.einsum("ktj,jd->td", table, back, preferred_element_type=jnp.float32)
        weighted = d_norm * gain_row
        result = (
            grad_out.astype(jnp.float32)
            + scale * weighted
            - values * (scale * scale * scale) * jnp.mean(values * weighted, axis=-1, keepdims=True)
        )
        return result.astype(jnp.bfloat16)

    def backward_tick(carry, tick):
        incoming, results = carry
        offset = tick - (sections - 1 - section)
        live = (offset >= 0) & (offset < micro)
        index = jnp.clip(offset, 0, micro - 1)
        slot = jnp.where(live, offset, micro)
        fresh = lax.dynamic_index_in_dim(cotangent, index, 0, keepdims=False)
        grad_out = jnp.where(section == sections - 1, fresh, incoming)
        tokens = lax.dynamic_index_in_dim(kept_x, index, 0, keepdims=False)
        table = lax.dynamic_index_in_dim(all_tables, index, 0, keepdims=False)
        scales4 = lax.dynamic_index_in_dim(all_scales4, index, 0, keepdims=False)
        gate_kept = lax.dynamic_index_in_dim(kept_gate, index, 0, keepdims=False)
        up_kept = lax.dynamic_index_in_dim(kept_up, index, 0, keepdims=False)
        result = backward_work(
            tokens, grad_out, table, scales4, gate_kept, up_kept, live
        )
        results = lax.dynamic_update_index_in_dim(results, result, slot, 0)
        incoming = passed_along(result, "section", -1)
        return ((incoming, results), None)

    done, _ = lax.scan(
        backward_tick,
        (
            jnp.zeros((tok, width), jnp.bfloat16),
            jnp.zeros(spare + cotangent.shape[1:], jnp.bfloat16),
        ),
        jnp.arange(ticks, dtype=jnp.int32),
    )
    results = done[1]
    return (outputs[None, :micro], results[None, :micro])


def solution(mesh):
    placed = (
        P(None, "expert", None),
        P(None, "expert", None),
        P("section", None),
        P("section", None, "expert", None),
        P("section", None, "expert", None),
        P("section", "expert", None, None),
        P("section", "expert", None, None),
        P("section", "expert", None, None),
    )
    return jax.shard_map(
        local,
        mesh=mesh,
        in_specs=placed,
        out_specs=(P("section", None, "expert", None), P("section", None, "expert", None)),
        check_vma=False,
    )
```

```python
import jax
import jax.numpy as jnp
from jax import lax
from jax.sharding import PartitionSpec as P

EPS = 1e-06


def passed_along(value, axis, steps):
    count = lax.axis_size(axis)
    leading, last = (max(0, -steps), min(count, count - steps))
    return lax.ppermute(value, axis, [(source, source + steps) for source in range(leading, last)])


def slot_places(route, experts, capacity):
    flat = route.reshape(-1)
    onehot = (flat[:, None] == jnp.arange(experts, dtype=jnp.int32)[None, :]).astype(jnp.int32)
    before = jnp.cumsum(onehot, axis=0) - onehot
    slot = jnp.sum(before * onehot, axis=1)
    return (flat * capacity + slot).reshape(route.shape)


def slot_table(places, total_rows):
    grid = jnp.arange(total_rows, dtype=jnp.int32)
    return (places.T[:, :, None] == grid[None, None, :]).astype(jnp.bfloat16)


def normalize(tokens, gain):
    values = tokens.astype(jnp.float32)
    scale = lax.rsqrt(jnp.mean(values * values, axis=-1, keepdims=True) + EPS)
    return (values, scale, (values * scale * gain).astype(jnp.bfloat16))


def pre_products(rows, w_gate, w_up):
    flat = rows.reshape(-1, rows.shape[-1])
    pre_gate = jnp.dot(flat, w_gate, preferred_element_type=jnp.float32)
    pre_up = jnp.dot(flat, w_up, preferred_element_type=jnp.float32)
    inner = rows.shape[:-1] + (w_gate.shape[1],)
    return (pre_gate.reshape(inner), pre_up.reshape(inner))


def expert_forward(rows, w_gate, w_up, w_down):
    pre_gate, pre_up = pre_products(rows, w_gate, w_up)
    width = w_gate.shape[1]
    product = (pre_gate * jax.nn.sigmoid(pre_gate) * pre_up).astype(jnp.bfloat16)
    output = jnp.dot(product.reshape(-1, width), w_down, preferred_element_type=jnp.float32).astype(
        jnp.bfloat16
    )
    return (output.reshape(rows.shape), pre_gate, pre_up)


def contract_last(left, right):
    return lax.dot_general(
        left, right, (((1,), (1,)), ((), ())), preferred_element_type=jnp.float32
    )


def expert_backward(grad_rows, pre_gate, pre_up, w_gate, w_up, w_down):
    shape = grad_rows.shape
    width = w_gate.shape[1]
    flat = grad_rows.reshape(-1, shape[-1])
    gate_pre = pre_gate.reshape(-1, width)
    up_pre = pre_up.reshape(-1, width)
    d_hidden = contract_last(flat, w_down)
    sigma = jax.nn.sigmoid(gate_pre)
    d_gate = (d_hidden * up_pre * sigma * (1.0 + gate_pre * (1.0 - sigma))).astype(jnp.bfloat16)
    d_up = (d_hidden * gate_pre * sigma).astype(jnp.bfloat16)
    back = contract_last(d_gate, w_gate) + contract_last(d_up, w_up)
    return back.astype(jnp.bfloat16).reshape(shape)


def return_rows(rows):
    return lax.all_to_all(rows, "expert", split_axis=0, concat_axis=0, tiled=True)


def local(inputs, cotangent, gain, route, gate, w_gate, w_up, w_down):
    micro, tok, width = inputs.shape
    top = route.shape[-1]
    experts = lax.axis_size("expert")
    capacity = tok * top * 7 // (6 * experts)
    total_rows = experts * capacity
    sections = lax.axis_size("section")
    section = lax.axis_index("section")
    ticks = sections + micro - 1
    gain_row = gain[0]
    weight_gate = w_gate[0, 0]
    weight_up = w_up[0, 0]
    weight_down = w_down[0, 0]
    inner = weight_gate.shape[1]
    routes = route[0]
    gates = gate[0]

    all_places = jax.vmap(lambda r: slot_places(r, experts, capacity))(routes)
    all_tables = jax.vmap(lambda p: slot_table(p, total_rows))(all_places)
    all_weights = jnp.einsum(
        "mktj,mtk->mtj", all_tables.astype(jnp.float32), gates, precision=lax.Precision.HIGHEST
    )
    all_tables4 = all_tables.reshape(micro, top, tok, experts, capacity)

    def forward_work(tokens, table4, weights, live):
        values, scale, normed = normalize(tokens, gain_row)
        send = jnp.einsum(
            "ktec,td->ecd", table4, normed, preferred_element_type=jnp.float32
        ).astype(jnp.bfloat16)

        def forward_active(operand):
            pre_gate, pre_up = pre_products(operand, weight_gate, weight_up)
            product = (pre_gate * jax.nn.sigmoid(pre_gate) * pre_up).astype(jnp.bfloat16)
            output = jnp.einsum(
                "ech,hd->ecd", product, weight_down, preferred_element_type=jnp.float32
            ).astype(jnp.bfloat16)
            return (output, pre_gate, pre_up)

        def forward_resting(operand):
            pre_zero = jnp.zeros(operand.shape[:-1] + (inner,), jnp.float32)
            return (jnp.zeros_like(operand), pre_zero, pre_zero)

        output, pre_gate, pre_up = lax.cond(
            live,
            forward_active,
            forward_resting,
            lax.all_to_all(send, "expert", split_axis=0, concat_axis=0, tiled=True),
        )
        back = return_rows(output).reshape(total_rows, width)
        mixed = values + jnp.dot(
            weights, back.astype(jnp.float32), precision=lax.Precision.HIGHEST
        )
        return (mixed.astype(jnp.bfloat16), pre_gate, pre_up)

    def forward_tick(carry, tick):
        incoming, outputs, kept_x, kept_gate, kept_up = carry
        offset = tick - section
        live = (offset >= 0) & (offset < micro)
        index = jnp.clip(offset, 0, micro - 1)
        slot = jnp.where(live, offset, micro)
        tokens = lax.cond(
            section == 0,
            lambda: lax.dynamic_index_in_dim(inputs, index, 0, keepdims=False),
            lambda: incoming,
        )
        table4 = lax.dynamic_index_in_dim(all_tables4, index, 0, keepdims=False)
        weights = lax.dynamic_index_in_dim(all_weights, index, 0, keepdims=False)
        mixed, pre_gate, pre_up = forward_work(tokens, table4, weights, live)
        outputs = lax.dynamic_update_index_in_dim(outputs, mixed, slot, 0)
        kept_x = lax.dynamic_update_index_in_dim(kept_x, tokens, slot, 0)
        kept_gate = lax.dynamic_update_index_in_dim(
            kept_gate, pre_gate.reshape(total_rows, inner), slot, 0
        )
        kept_up = lax.dynamic_update_index_in_dim(
            kept_up, pre_up.reshape(total_rows, inner), slot, 0
        )
        incoming = passed_along(mixed, "section", 1)
        return ((incoming, outputs, kept_x, kept_gate, kept_up), None)

    spare = (micro + 1,)
    start = (
        jnp.zeros((tok, width), jnp.bfloat16),
        jnp.zeros(spare + inputs.shape[1:], jnp.bfloat16),
        jnp.zeros(spare + inputs.shape[1:], jnp.bfloat16),
        jnp.zeros(spare + (total_rows, inner), jnp.float32),
        jnp.zeros(spare + (total_rows, inner), jnp.float32),
    )
    finished, _ = lax.scan(forward_tick, start, jnp.arange(ticks, dtype=jnp.int32))
    _, outputs, kept_x, kept_gate, kept_up = finished
    down_across = lax.optimization_barrier(jnp.transpose(weight_down))

    def backward_work(tokens, grad_out, table, table4, gate_now, gate_kept, up_kept, live):
        values, scale, normed = normalize(tokens, gain_row)
        scaled = (gate_now[..., None] * grad_out.astype(jnp.float32)[:, None, :]).astype(
            jnp.bfloat16
        )
        grad_send = jnp.einsum(
            "ktec,tkd->ecd", table4, scaled, preferred_element_type=jnp.float32
        ).astype(jnp.bfloat16)

        def backward_active(operands):
            rows_grad, gate_pre, up_pre = operands
            d_hidden = jnp.dot(
                rows_grad.reshape(total_rows, width),
                down_across,
                preferred_element_type=jnp.float32,
            )
            sigma = jax.nn.sigmoid(gate_pre)
            d_gate = (d_hidden * up_pre * sigma * (1.0 + gate_pre * (1.0 - sigma))).astype(
                jnp.bfloat16
            )
            d_up = (d_hidden * gate_pre * sigma).astype(jnp.bfloat16)
            back = contract_last(d_gate, weight_gate) + contract_last(d_up, weight_up)
            return back.astype(jnp.bfloat16).reshape(rows_grad.shape)

        def backward_resting(operands):
            return jnp.zeros_like(operands[0])

        computed = lax.cond(
            live,
            backward_active,
            backward_resting,
            (
                lax.all_to_all(grad_send, "expert", split_axis=0, concat_axis=0, tiled=True),
                gate_kept,
                up_kept,
            ),
        )
        back = return_rows(computed).reshape(total_rows, width)
        d_norm = jnp.einsum("ktj,jd->td", table, back, preferred_element_type=jnp.float32)
        weighted = d_norm * gain_row
        result = (
            grad_out.astype(jnp.float32)
            + scale * weighted
            - values * (scale * scale * scale) * jnp.mean(values * weighted, axis=-1, keepdims=True)
        )
        return result.astype(jnp.bfloat16)

    def backward_tick(carry, tick):
        incoming, results = carry
        offset = tick - (sections - 1 - section)
        live = (offset >= 0) & (offset < micro)
        index = jnp.clip(offset, 0, micro - 1)
        slot = jnp.where(live, offset, micro)
        grad_out = lax.cond(
            section == sections - 1,
            lambda: lax.dynamic_index_in_dim(cotangent, index, 0, keepdims=False),
            lambda: incoming,
        )
        tokens = lax.dynamic_index_in_dim(kept_x, index, 0, keepdims=False)
        table = lax.dynamic_index_in_dim(all_tables, index, 0, keepdims=False)
        table4 = lax.dynamic_index_in_dim(all_tables4, index, 0, keepdims=False)
        gate_now = lax.dynamic_index_in_dim(gates, index, 0, keepdims=False)
        gate_kept = lax.dynamic_index_in_dim(kept_gate, index, 0, keepdims=False)
        up_kept = lax.dynamic_index_in_dim(kept_up, index, 0, keepdims=False)
        result = backward_work(
            tokens, grad_out, table, table4, gate_now, gate_kept, up_kept, live
        )
        results = lax.dynamic_update_index_in_dim(results, result, slot, 0)
        incoming = passed_along(result, "section", -1)
        return ((incoming, results), None)

    done, _ = lax.scan(
        backward_tick,
        (
            jnp.zeros((tok, width), jnp.bfloat16),
            jnp.zeros(spare + cotangent.shape[1:], jnp.bfloat16),
        ),
        jnp.arange(ticks, dtype=jnp.int32),
    )
    results = done[1]
    return (outputs[None, :micro], results[None, :micro])


def solution(mesh):
    placed = (
        P(None, "expert", None),
        P(None, "expert", None),
        P("section", None),
        P("section", None, "expert", None),
        P("section", None, "expert", None),
        P("section", "expert", None, None),
        P("section", "expert", None, None),
        P("section", "expert", None, None),
    )
    return jax.shard_map(
        local,
        mesh=mesh,
        in_specs=placed,
        out_specs=(P("section", None, "expert", None), P("section", None, "expert", None)),
        check_vma=False,
    )
```
